128 devices in a mesh: seq: 16 (over x, z_lo, core), heads: 8 (over z_hi, y).
Axes of the slice: x: 4, y: 4, z: 4 (z_hi: 2, z_lo: 2; z = z_hi * 2 + z_lo), core: 2. Of those that a mesh axis runs over, the one named last changes fastest.
Arguments:
- tokens: bfloat16 [4096, 5120], P('seq', 'heads'), may hold values from -6 to 6
- order: int32 [4096], replicated, may hold values from 0 to 4095, each once
- lengths: int32 [12], replicated, may hold values from 1 to 1024, 4096 in all
- block_table: int32 [12, 2], replicated, may hold values from 0 to 31, as said below
- destination: int32 [32], replicated, may hold values from 0 to 31, each once
- w_query: bfloat16 [5120, 5120], P(None, 'heads'), may hold values from -0.078125 to 0.078125
- key_weight: bfloat16 [5120, 1024], P(None, 'heads'), may hold values from -0.078125 to 0.078125
- value_weight: bfloat16 [5120, 1024], P(None, 'heads'), may hold values from -0.078125 to 0.078125
- w_out: bfloat16 [5120, 5120], P('heads'), may hold values from -0.078125 to 0.078125
- key_value_cache: bfloat16 [4, 32, 512, 2, 1024], P(None, None, 'seq', None, 'heads'), may hold values from -600 to 600
Outputs:
- attn_out: bfloat16 [4096, 5120], P('seq', 'heads')
- decode_cache: bfloat16 [4, 32, 512, 2, 1024], P(None, 'seq', None, None, 'heads')
The draws below stay inside these ranges and needn't reach their ends.
Inputs may be any that keep to these rules, and one draw needn't show every extreme that they name: `block_table`: each of the 12 requests names 2 blocks; no block is named twice.
All inputs are finite; a program needn't handle non-finite values.
Results may differ from the reference program's by a relative error of at most 0.015.
The reference program's roundings to bfloat16 on the way count: a program that leaves them out, or rounds other values in their place, can miss the bound.
Values may be sent and summed in bfloat16 or wider, within the bound.
No kernel may reach another device: no remote copies, remote signals or barrier semaphores. Data moves between devices by JAX's collectives and lax.ppermute only.
A program may use at most 128 MiB of HBM per device.

```python
import math
import jax
import jax.numpy as jnp
import numpy as np
from jax import lax

MODEL_WIDTH = 5120
QUERY_HEADS = 40
KEY_VALUE_HEADS = 8
HEAD_SIZE = 128
BLOCK_POSITIONS = 512
CB = 2
REQS = 12
POOL_BLOCKS = 32
HANDOVER_LAYERS = 4
NEW_TOKENS = 4096


def draw_block_table(key, part):
    mixed = jax.random.permutation(key, POOL_BLOCKS)
    return mixed[:REQS * CB].reshape(REQS, CB).astype(jnp.int32)


def draw_key_value_cache(key, part):
    array_shape = (HANDOVER_LAYERS, POOL_BLOCKS, BLOCK_POSITIONS, 2, KEY_VALUE_HEADS * HEAD_SIZE)
    first = jax.random.fold_in(jax.random.fold_in(key, 7), 0)
    result = jnp.clip(jax.random.normal(first, array_shape, jnp.float32), -6.0, 6.0)
    return result.astype(jnp.bfloat16)


def block_levels(own_key, shape, cuts, low, high):
    gain = 1.0
    for axis_at, shards_of in cuts:
        draws = jax.random.uniform(jax.random.fold_in(jax.random.fold_in(own_key, 6), axis_at), (shards_of,), jnp.float32, low / len(cuts), high / len(cuts))
        gain = gain * jnp.repeat(jnp.exp(draws), shape[axis_at] // shards_of).reshape((-1,) + (1,) * (len(shape) - 1 - axis_at))
    return gain


def length_profile(amount, total, bound, lean):
    loads = [(1 << 20) // math.isqrt(rank ** lean) + 1 for rank in range(2, amount + 1)]
    spare, given = total - bound - (amount - 1), [1] * (amount - 1)
    while spare > 0:
        movable = [i for i in range(amount - 1) if given[i] < bound]
        pool, budget = sum([loads[i] for i in movable]), spare
        for i in movable:
            addition = min(bound - given[i], max(1, budget * loads[i] // pool), spare)
            given[i] = given[i] + addition
            spare = spare - addition
    return np.array([bound] + given)


def uneven_parts(rng, count, total, reach, skew):
    if count == 2:
        one = jax.random.randint(rng, (), max(1, total - reach), min(reach, total - 1) + 1)
        return jnp.stack([one, total - one])
    sizes = jnp.asarray(length_profile(count, total, reach, skew), jnp.int32)
    twos = (count - 1) // 2
    source_of, taker = sizes[1:1 + 2 * twos:2], sizes[2:2 + 2 * twos:2]
    room = jnp.minimum(source_of - 1, reach - taker)
    shifted = jax.random.randint(jax.random.fold_in(rng, 1), (twos,), 0, 1 << 20) % (room + 1)
    sizes = sizes.at[1:1 + 2 * twos:2].set(source_of - shifted).at[2:2 + 2 * twos:2].set(taker + shifted)
    return sizes[jax.random.permutation(jax.random.fold_in(rng, 2), count)]


def bell_draw(stream_key, shape, scale, most, shards=(), kind=jnp.bfloat16):
    values = jax.random.normal(stream_key, shape, jnp.float32) * scale
    if len(shards) > 0:
        values = block_levels(stream_key, shape, shards, -0.22, 0.18) * values
    return jnp.clip(values, min=-most, max=most).astype(kind)


def setup_inputs(seed: int = 0) -> dict:
    key_of = jax.random.split(jax.random.key(seed), 11)
    tokens = bell_draw(key_of[0], (NEW_TOKENS, MODEL_WIDTH), 1.0, 6.0, ((0, 16), (1, 8)))
    order = jax.random.permutation(key_of[1], NEW_TOKENS).astype(jnp.int32)
    lengths = uneven_parts(key_of[2], REQS, NEW_TOKENS, NEW_TOKENS // 4, 2).astype(jnp.int32)
    block_table = draw_block_table(jax.random.fold_in(key_of[10], 71), 0)
    destination = jax.random.permutation(key_of[4], POOL_BLOCKS).astype(jnp.int32)
    w_query = bell_draw(key_of[5], (MODEL_WIDTH, QUERY_HEADS * HEAD_SIZE), MODEL_WIDTH ** -0.5, 0.078125, ((1, 8),))
    key_weight = bell_draw(key_of[6], (MODEL_WIDTH, KEY_VALUE_HEADS * HEAD_SIZE), MODEL_WIDTH ** -0.5, 0.078125, ((1, 8),))
    value_weight = bell_draw(key_of[7], (MODEL_WIDTH, KEY_VALUE_HEADS * HEAD_SIZE), MODEL_WIDTH ** -0.5, 0.078125, ((1, 8),))
    w_out = bell_draw(key_of[8], (QUERY_HEADS * HEAD_SIZE, MODEL_WIDTH), (QUERY_HEADS * HEAD_SIZE) ** -0.5, 0.078125, ((0, 8),))
    key_value_cache = draw_key_value_cache(jax.random.fold_in(key_of[10], 71), 0)
    return dict(tokens=tokens, order=order, lengths=lengths, block_table=block_table, destination=destination, w_query=w_query, key_weight=key_weight, value_weight=value_weight, w_out=w_out, key_value_cache=key_value_cache)


theta = 1000000.0
epsilon = 1e-06

def apply_rotary(value_rows, place):
    half = value_rows.shape[-1] // 2
    freq = theta ** (-2.0 * jnp.arange(half, dtype=jnp.float32) / value_rows.shape[-1])
    angle = place[:, None, None] * freq
    cosine = jnp.cos(angle)
    sine_part = jnp.sin(angle)
    first = value_rows[..., :half]
    second = value_rows[..., half:]
    return jnp.concatenate([first * cosine - second * sine_part, second * cosine + first * sine_part], axis=-1)

def request_place(order, lengths):
    ends = jnp.cumsum(lengths).astype(jnp.int32)
    starts = ends - lengths
    request = lax.optimization_barrier(jnp.sum((order[:, None] >= ends[None, :]).astype(jnp.int32), axis=1)).astype(jnp.int32)
    labels = jnp.arange(lengths.shape[0], dtype=jnp.int32)
    begin = lax.optimization_barrier(jnp.sum(jnp.where(request[:, None] == labels[None, :], starts[None, :], 0), axis=1)).astype(jnp.int32)
    return (request, (order - begin).astype(jnp.int32))

def reference(tokens, order, lengths, block_table, destination, w_query, key_weight, value_weight, w_out, key_value_cache):
    wide = tokens.astype(jnp.float32)
    normed = (wide * lax.rsqrt(lax.optimization_barrier(jnp.mean(wide * wide, axis=1, keepdims=True)) + epsilon)).astype(jnp.bfloat16)
    query_rows = jnp.dot(normed, w_query, preferred_element_type=jnp.float32)
    key_rows = jnp.dot(normed, key_weight, preferred_element_type=jnp.float32)
    value_rows = jnp.dot(normed, value_weight, preferred_element_type=jnp.float32)
    request, position = request_place(order, lengths)
    rotary_angles = (position + CB * BLOCK_POSITIONS).astype(jnp.float32)
    head_group = QUERY_HEADS // KEY_VALUE_HEADS
    query_rows = apply_rotary(query_rows.reshape(NEW_TOKENS, QUERY_HEADS, HEAD_SIZE), rotary_angles).astype(jnp.bfloat16).reshape(NEW_TOKENS, KEY_VALUE_HEADS, head_group, HEAD_SIZE)
    key_rows = apply_rotary(key_rows.reshape(NEW_TOKENS, KEY_VALUE_HEADS, HEAD_SIZE), rotary_angles).astype(jnp.bfloat16)
    value_rows = value_rows.reshape(NEW_TOKENS, KEY_VALUE_HEADS, HEAD_SIZE).astype(jnp.bfloat16)
    cache_lookup = key_value_cache[0].reshape(POOL_BLOCKS, BLOCK_POSITIONS, 2, KEY_VALUE_HEADS, HEAD_SIZE)
    scale = HEAD_SIZE ** (-0.5)
    span = 512 if NEW_TOKENS % 512 == 0 else NEW_TOKENS

    def single_head(head):
        head_keys = lax.dynamic_index_in_dim(key_rows, head, 1, keepdims=False).astype(jnp.float32)
        head_values = lax.dynamic_index_in_dim(value_rows, head, 1, keepdims=False).astype(jnp.float32)
        head_query = lax.dynamic_index_in_dim(query_rows, head, 1, keepdims=False)
        head_cache = lax.dynamic_index_in_dim(cache_lookup, head, 3, keepdims=False)

        def one_block(index):
            start = (index * span).astype(jnp.int32)
            block_query = lax.dynamic_slice_in_dim(head_query, start, span, 0).astype(jnp.float32)
            block_request = lax.dynamic_slice_in_dim(request, start, span, 0)
            block_position = lax.dynamic_slice_in_dim(position, start, span, 0)
            chosen = head_cache[block_table[block_request]].reshape(span, CB * BLOCK_POSITIONS, 2, HEAD_SIZE)
            cache_keys = chosen[:, :, 0].astype(jnp.float32)
            cache_values = chosen[:, :, 1].astype(jnp.float32)
            cache_scores = jnp.einsum('qah,qkh->qak', block_query, cache_keys) * scale
            fresh_scores = jnp.einsum('qah,kh->qak', block_query, head_keys) * scale
            allowed = (request[None, :] == block_request[:, None]) & (position[None, :] <= block_position[:, None])
            fresh_scores = jnp.where(allowed[:, None, :], fresh_scores, -jnp.inf)
            top = jnp.maximum(lax.optimization_barrier(jnp.max(cache_scores, axis=-1)), lax.optimization_barrier(jnp.max(fresh_scores, axis=-1)))
            cache_expo = jnp.exp(cache_scores - top[..., None])
            fresh_expo = jnp.exp(fresh_scores - top[..., None])
            total = lax.optimization_barrier(jnp.sum(cache_expo, axis=-1)) + lax.optimization_barrier(jnp.sum(fresh_expo, axis=-1))
            cache_weights = cache_expo.astype(jnp.bfloat16).astype(jnp.float32)
            fresh_weights = fresh_expo.astype(jnp.bfloat16).astype(jnp.float32)
            weighted = jnp.einsum('qak,qkh->qah', cache_weights, cache_values)
            weighted = weighted + jnp.einsum('qak,kh->qah', fresh_weights, head_values)
            return weighted / total[..., None]
        result = lax.map(one_block, jnp.arange(NEW_TOKENS // span, dtype=jnp.int32))
        return result.reshape(NEW_TOKENS, head_group, HEAD_SIZE)
    head_outputs = lax.map(single_head, jnp.arange(KEY_VALUE_HEADS, dtype=jnp.int32))
    attn = jnp.transpose(head_outputs, (1, 0, 2, 3)).reshape(NEW_TOKENS, QUERY_HEADS * HEAD_SIZE).astype(jnp.bfloat16)
    attn_out = jnp.dot(attn, w_out, preferred_element_type=jnp.float32).astype(jnp.bfloat16)
    source = jnp.zeros((POOL_BLOCKS,), jnp.int32).at[destination].set(jnp.arange(POOL_BLOCKS, dtype=jnp.int32))
    decode_cache = key_value_cache[:, source]
    return (attn_out, decode_cache)
```

```python
import jax
import jax.numpy as jnp
from jax import lax
from jax.sharding import PartitionSpec as P

QUERY_HEADS = 40
KEY_VALUE_HEADS = 8
HEAD_SIZE = 128
BLOCK_POSITIONS = 512
CB = 2


theta = 1000000.0
epsilon = 1e-06


def apply_rotary(value_rows, place):
    half = value_rows.shape[-1] // 2
    freq = theta ** (-2.0 * jnp.arange(half, dtype=jnp.float32) / value_rows.shape[-1])
    angle = place[:, None, None] * freq
    cosine = jnp.cos(angle)
    sine_part = jnp.sin(angle)
    first = value_rows[..., :half]
    second = value_rows[..., half:]
    return jnp.concatenate(
        [first * cosine - second * sine_part, second * cosine + first * sine_part], axis=-1
    )


def request_place(order, lengths):
    ends = jnp.cumsum(lengths)
    starts = ends - lengths
    request = jnp.sum((order[:, None] >= ends[None, :]).astype(jnp.int32), axis=1)
    labels = jnp.arange(lengths.shape[0], dtype=jnp.int32)
    begin = jnp.sum(jnp.where(request[:, None] == labels[None, :], starts[None, :], 0), axis=1)
    return (request, order - begin)


def group_span(count, limit):
    span = min(count, limit)
    while count % span != 0:
        span -= 1
    return span


def attend(carry, query_rows, request, position, piece, key_request, key_position):
    count = piece.shape[0]
    span = group_span(count, 2048)
    steps = count // span
    pieces = piece.reshape(steps, span, piece.shape[1], piece.shape[2], piece.shape[3])
    requests = key_request.reshape(steps, span)
    positions = key_position.reshape(steps, span)
    scale = query_rows.shape[-1] ** (-0.5)

    def one_group(state, items):
        top, total, accum = state
        block, block_request, block_position = items
        scores = (
            jnp.einsum(
                "qgah,kgh->qgak", query_rows, block[:, 0], preferred_element_type=jnp.float32
            )
            * scale
        )
        allowed = (block_request[None, :] == request[:, None]) & (
            block_position[None, :] <= position[:, None]
        )
        wide_mask = allowed[:, None, None, :]
        row_max = jnp.max(jnp.where(wide_mask, scores, -1e30), axis=-1)
        new_top = jnp.maximum(top, row_max)
        expo = jnp.where(wide_mask, jnp.exp(scores - new_top[..., None]), 0.0)
        fade = jnp.exp(top - new_top)
        total = total * fade + jnp.sum(expo, axis=-1)
        weights = expo.astype(jnp.bfloat16)
        accum = accum * fade[..., None] + jnp.einsum(
            "qgak,kgh->qgah", weights, block[:, 1], preferred_element_type=jnp.float32
        )
        return ((new_top, total, accum), None)

    carry, unused = lax.scan(one_group, carry, (pieces, requests, positions))
    return carry


def hand_over(arranged, device):
    parts = lax.psum(1, "seq")
    layers, slots = arranged.shape[0], arranged.shape[1]
    width = slots // parts
    chunks = arranged.reshape(layers, parts, width, *arranged.shape[2:])
    received = []
    for shift in range(parts):
        target = lax.rem(device + shift, parts)
        chunk = lax.dynamic_index_in_dim(chunks, target, 1, keepdims=False)
        if shift > 0:
            pairs = [(i, (i + shift) % parts) for i in range(parts)]
            chunk = lax.ppermute(chunk, "seq", pairs)
        received.append(chunk)
    stacked = jnp.stack(received, axis=2)
    sources = lax.rem(device - jnp.arange(parts, dtype=jnp.int32) + parts, parts)
    placed = jnp.take(stacked, sources, axis=2)
    return placed.reshape(layers, width, parts * arranged.shape[2], *arranged.shape[3:])


def on_device(
    tokens,
    order,
    lengths,
    block_table,
    destination,
    w_query,
    key_weight,
    value_weight,
    w_out,
    key_value_cache,
):
    full = lax.all_gather(tokens, "heads", axis=1, tiled=True)
    rows = full.shape[0]
    wide = full.astype(jnp.float32)
    normed = (wide * lax.rsqrt(jnp.mean(wide * wide, axis=1, keepdims=True) + epsilon)).astype(
        jnp.bfloat16
    )
    local_heads = key_weight.shape[1] // HEAD_SIZE
    head_group = QUERY_HEADS // KEY_VALUE_HEADS
    query_rows = jnp.dot(normed, w_query, preferred_element_type=jnp.float32)
    key_rows = jnp.dot(normed, key_weight, preferred_element_type=jnp.float32)
    value_rows = jnp.dot(normed, value_weight, preferred_element_type=jnp.float32)
    device = lax.axis_index("seq")
    my_order = lax.dynamic_slice_in_dim(order, device * rows, rows)
    request, position = request_place(my_order, lengths)
    rotary_angles = (position + CB * BLOCK_POSITIONS).astype(jnp.float32)
    query_rows = apply_rotary(
        query_rows.reshape(rows, local_heads * head_group, HEAD_SIZE), rotary_angles
    ).astype(jnp.bfloat16)
    query_rows = query_rows.reshape(rows, local_heads, head_group, HEAD_SIZE)
    key_rows = (
        apply_rotary(key_rows.reshape(rows, local_heads, HEAD_SIZE), rotary_angles)
        .astype(jnp.bfloat16)
        .reshape(rows, local_heads * HEAD_SIZE)
    )
    packed = jnp.stack([key_rows, value_rows.astype(jnp.bfloat16)], axis=1)
    initial = (
        jnp.full((rows, local_heads, head_group), -1e30, jnp.float32),
        jnp.zeros((rows, local_heads, head_group), jnp.float32),
        jnp.zeros((rows, local_heads, head_group, HEAD_SIZE), jnp.float32),
    )
    piece = lax.all_gather(packed, "seq", axis=0, tiled=True)
    count = piece.shape[0]
    key_request, key_position = request_place(order, lengths)
    state = attend(
        initial,
        query_rows,
        request,
        position,
        piece.reshape(count, 2, local_heads, HEAD_SIZE),
        key_request,
        key_position,
    )
    layer_zero = key_value_cache[0]
    used = jnp.take(layer_zero, block_table.reshape(-1), axis=0)
    piece = lax.all_gather(used, "seq", axis=1, tiled=True)
    blocks = piece.shape[0]
    count = piece.shape[1]
    owner = jnp.arange(blocks, dtype=jnp.int32) // block_table.shape[1]
    key_request = jnp.repeat(owner, count)
    key_position = jnp.full((blocks * count,), -1, jnp.int32)
    flat = piece.reshape(blocks * count, 2, local_heads, HEAD_SIZE)
    state = attend(state, query_rows, request, position, flat, key_request, key_position)
    top, total, accum = state
    attn = (
        (accum / total[..., None])
        .astype(jnp.bfloat16)
        .reshape(rows, local_heads * head_group * HEAD_SIZE)
    )
    partial_value = jnp.dot(attn, w_out, preferred_element_type=jnp.float32)
    attn_out = lax.psum_scatter(
        partial_value.astype(jnp.bfloat16), "heads", scatter_dimension=1, tiled=True
    )
    slots = destination.shape[0]
    slot_labels = jnp.arange(slots, dtype=jnp.int32)
    inverse = jnp.sum(
        jnp.where(destination[None, :] == slot_labels[:, None], slot_labels[None, :], 0), axis=1
    )
    arranged = jnp.take(key_value_cache, inverse, axis=1)
    decode_cache = hand_over(arranged, device)
    return (attn_out, decode_cache)


def solution(mesh):
    placed = (
        P("seq", "heads"),
        P(),
        P(),
        P(),
        P(),
        P(None, "heads"),
        P(None, "heads"),
        P(None, "heads"),
        P("heads", None),
        P(None, None, "seq", None, "heads"),
    )
    return jax.shard_map(
        on_device,
        mesh=mesh,
        in_specs=placed,
        out_specs=(P("seq", "heads"), P(None, "seq", None, None, "heads")),
        check_vma=False,
    )
```

```python
import jax
import jax.numpy as jnp
from jax import lax
from jax.sharding import PartitionSpec as P
import functools
from jax.experimental import pallas as pl
from jax.experimental.pallas import tpu as pltpu

QUERY_HEADS = 40
KEY_VALUE_HEADS = 8
HEAD_SIZE = 128
BLOCK_POSITIONS = 512
CB = 2


theta = 1000000.0
epsilon = 1e-06


def apply_rotary(value_rows, place):
    half = value_rows.shape[-1] // 2
    freq = theta ** (-2.0 * jnp.arange(half, dtype=jnp.float32) / value_rows.shape[-1])
    angle = place[:, None, None] * freq
    cosine = jnp.cos(angle)
    sine_part = jnp.sin(angle)
    first = value_rows[..., :half]
    second = value_rows[..., half:]
    return jnp.concatenate(
        [first * cosine - second * sine_part, second * cosine + first * sine_part], axis=-1
    )


def request_place(order, lengths):
    ends = jnp.cumsum(lengths)
    starts = ends - lengths
    request = jnp.sum((order[:, None] >= ends[None, :]).astype(jnp.int32), axis=1)
    labels = jnp.arange(lengths.shape[0], dtype=jnp.int32)
    begin = jnp.sum(jnp.where(request[:, None] == labels[None, :], starts[None, :], 0), axis=1)
    return (request, order - begin)


from jax.experimental import pallas as pl
from jax.experimental.pallas import tpu as pltpu

TILE = 32
CHUNK = 256


def _attn_body(tables, q_ref, o_ref, rs_ref, req_ref, kv_ref, cache_ref, out_ref, *, group, scale):
    t = pl.program_id(0)
    rows = q_ref.shape[1]
    size = q_ref.shape[2]
    q = q_ref[...].reshape(group * rows, size)
    o_row = o_ref[...]
    rs_row = rs_ref[...]
    req_row = req_ref[...]

    def update(carry, keys, values, mask):
        top, total, accum = carry
        width = keys.shape[0]
        scores = lax.dot_general(q, keys, (((1,), (1,)), ((), ())), preferred_element_type=jnp.float32) * scale
        scores = scores.reshape(group, rows, width)
        scores = jnp.where(mask[None], scores, -1e30).reshape(group * rows, width)
        new_top = jnp.maximum(top, jnp.max(scores, axis=1, keepdims=True))
        expo = jnp.exp(scores - new_top).reshape(group, rows, width)
        expo = jnp.where(mask[None], expo, 0.0).reshape(group * rows, width)
        fade = jnp.exp(top - new_top)
        total = total * fade + jnp.sum(expo, axis=1, keepdims=True)
        accum = accum * fade + jnp.dot(expo.astype(jnp.bfloat16), values, preferred_element_type=jnp.float32)
        return (new_top, total, accum)

    def cached(r, carry):
        mask = req_row == r
        for j in range(2):
            block = cache_ref[2 * r + j]
            carry = update(carry, block[:, :size], block[:, size:], mask)
        return carry

    def fresh(c, carry):
        start = pl.multiple_of(c * CHUNK, CHUNK)
        block = kv_ref[pl.ds(start, CHUNK), :]
        index = start + lax.broadcasted_iota(jnp.int32, (1, CHUNK), 1)
        mask = (index >= rs_row) & (index <= o_row)
        return update(carry, block[:, :size], block[:, size:], mask)

    carry = (
        jnp.full((group * rows, 1), -1e30, jnp.float32),
        jnp.zeros((group * rows, 1), jnp.float32),
        jnp.zeros((group * rows, size), jnp.float32),
    )
    carry = lax.fori_loop(tables[0, t], tables[1, t] + 1, cached, carry)
    carry = lax.fori_loop(tables[2, t], tables[3, t] + 1, fresh, carry)
    top, total, accum = carry
    out_ref[...] = (accum / total).reshape(group, rows, size).astype(out_ref.dtype)


def sparse_attention(q_sorted, o_sorted, rs_sorted, req_sorted, kv_sorted, cache, interpret=False):
    group, count, size = q_sorted.shape
    tiles = count // TILE
    firsts = jnp.arange(tiles) * TILE
    lasts = firsts + TILE - 1
    tables = jnp.stack([
        req_sorted[firsts], req_sorted[lasts], rs_sorted[firsts] // CHUNK, o_sorted[lasts] // CHUNK
    ]).astype(jnp.int32)
    col = lambda v: v.reshape(count, 1).astype(jnp.int32)
    body = functools.partial(_attn_body, group=group, scale=size ** (-0.5))
    spec = pltpu.PrefetchScalarGridSpec(
        num_scalar_prefetch=1,
        grid=(tiles,),
        in_specs=[
            pl.BlockSpec((group, TILE, size), lambda t, tb: (0, t, 0)),
            pl.BlockSpec((TILE, 1), lambda t, tb: (t, 0)),
            pl.BlockSpec((TILE, 1), lambda t, tb: (t, 0)),
            pl.BlockSpec((TILE, 1), lambda t, tb: (t, 0)),
            pl.BlockSpec(kv_sorted.shape, lambda t, tb: (0, 0)),
            pl.BlockSpec(cache.shape, lambda t, tb: (0, 0, 0)),
        ],
        out_specs=pl.BlockSpec((group, TILE, size), lambda t, tb: (0, t, 0)),
    )
    return pl.pallas_call(
        body,
        grid_spec=spec,
        out_shape=jax.ShapeDtypeStruct(q_sorted.shape, jnp.bfloat16),
        compiler_params=pltpu.CompilerParams(dimension_semantics=("arbitrary",)),
        interpret=interpret,
    )(tables, q_sorted, col(o_sorted), col(rs_sorted), col(req_sorted), kv_sorted, cache)


def hand_over(arranged, device):
    parts = lax.psum(1, "seq")
    layers, slots = arranged.shape[0], arranged.shape[1]
    width = slots // parts
    chunks = arranged.reshape(layers, parts, width, *arranged.shape[2:])
    received = []
    for shift in range(parts):
        target = lax.rem(device + shift, parts)
        chunk = lax.dynamic_index_in_dim(chunks, target, 1, keepdims=False)
        if shift > 0:
            pairs = [(i, (i + shift) % parts) for i in range(parts)]
            chunk = lax.ppermute(chunk, "seq", pairs)
        received.append(chunk)
    stacked = jnp.stack(received, axis=2)
    sources = lax.rem(device - jnp.arange(parts, dtype=jnp.int32) + parts, parts)
    placed = jnp.take(stacked, sources, axis=2)
    return placed.reshape(layers, width, parts * arranged.shape[2], *arranged.shape[3:])


def on_device(
    tokens,
    order,
    lengths,
    block_table,
    destination,
    w_query,
    key_weight,
    value_weight,
    w_out,
    key_value_cache,
):
    full = lax.all_gather(tokens, "heads", axis=1, tiled=True)
    rows = full.shape[0]
    wide = full.astype(jnp.float32)
    normed = (wide * lax.rsqrt(jnp.mean(wide * wide, axis=1, keepdims=True) + epsilon)).astype(
        jnp.bfloat16
    )
    local_heads = key_weight.shape[1] // HEAD_SIZE
    head_group = QUERY_HEADS // KEY_VALUE_HEADS
    query_rows = jnp.dot(normed, w_query, preferred_element_type=jnp.float32)
    key_rows = jnp.dot(normed, key_weight, preferred_element_type=jnp.float32)
    value_rows = jnp.dot(normed, value_weight, preferred_element_type=jnp.float32)
    device = lax.axis_index("seq")
    my_order = lax.dynamic_slice_in_dim(order, device * rows, rows)
    request, position = request_place(my_order, lengths)
    rotary_angles = (position + CB * BLOCK_POSITIONS).astype(jnp.float32)
    query_rows = apply_rotary(
        query_rows.reshape(rows, local_heads * head_group, HEAD_SIZE), rotary_angles
    ).astype(jnp.bfloat16)
    query_rows = query_rows.reshape(rows, local_heads, head_group, HEAD_SIZE)
    key_rows = (
        apply_rotary(key_rows.reshape(rows, local_heads, HEAD_SIZE), rotary_angles)
        .astype(jnp.bfloat16)
        .reshape(rows, local_heads * HEAD_SIZE)
    )
    fresh_rows = jnp.concatenate(
        [
            key_rows.reshape(rows, local_heads, HEAD_SIZE),
            value_rows.astype(jnp.bfloat16).reshape(rows, local_heads, HEAD_SIZE),
        ],
        axis=2,
    )
    gathered = lax.all_gather(fresh_rows, "seq", axis=0, tiled=True)
    kv_sorted = jnp.take(gathered, jnp.argsort(order), axis=0)
    layer_zero = key_value_cache[0]
    used = jnp.take(layer_zero, block_table.reshape(-1), axis=0)
    pool, span = used.shape[0], used.shape[1]
    used = used.reshape(pool, span, 2, local_heads, HEAD_SIZE).transpose(0, 1, 3, 2, 4)
    used = used.reshape(pool, span, local_heads, 2 * HEAD_SIZE)
    cache = lax.all_gather(used, "seq", axis=1, tiled=True)
    perm = jnp.argsort(my_order)
    o_sorted = jnp.take(my_order, perm)
    rs_sorted = jnp.take(my_order - position, perm)
    req_sorted = jnp.take(request, perm)
    q_sorted = jnp.take(query_rows, perm, axis=0)
    unsort = jnp.argsort(perm)
    outs = []
    for head in range(local_heads):
        result = sparse_attention(
            q_sorted[:, head].transpose(1, 0, 2),
            o_sorted,
            rs_sorted,
            req_sorted,
            kv_sorted[:, head],
            cache[:, :, head],
        )
        outs.append(jnp.take(result, unsort, axis=1).transpose(1, 0, 2))
    attn = jnp.stack(outs, axis=1).reshape(rows, local_heads * head_group * HEAD_SIZE)
    partial_value = jnp.dot(attn, w_out, preferred_element_type=jnp.float32)
    attn_out = lax.psum_scatter(
        partial_value.astype(jnp.bfloat16), "heads", scatter_dimension=1, tiled=True
    )
    slots = destination.shape[0]
    slot_labels = jnp.arange(slots, dtype=jnp.int32)
    inverse = jnp.sum(
        jnp.where(destination[None, :] == slot_labels[:, None], slot_labels[None, :], 0), axis=1
    )
    arranged = jnp.take(key_value_cache, inverse, axis=1)
    decode_cache = hand_over(arranged, device)
    return (attn_out, decode_cache)


def solution(mesh):
    placed = (
        P("seq", "heads"),
        P(),
        P(),
        P(),
        P(),
        P(None, "heads"),
        P(None, "heads"),
        P(None, "heads"),
        P("heads", None),
        P(None, None, "seq", None, "heads"),
    )
    return jax.shard_map(
        on_device,
        mesh=mesh,
        in_specs=placed,
        out_specs=(P("seq", "heads"), P(None, "seq", None, None, "heads")),
        check_vma=False,
    )
```

```python
import jax
import jax.numpy as jnp
from jax import lax
from jax.sharding import PartitionSpec as P
import functools
from jax.experimental import pallas as pl
from jax.experimental.pallas import tpu as pltpu

QUERY_HEADS = 40
KEY_VALUE_HEADS = 8
HEAD_SIZE = 128
BLOCK_POSITIONS = 512
CB = 2


theta = 1000000.0
epsilon = 1e-06


def apply_rotary(value_rows, place):
    half = value_rows.shape[-1] // 2
    freq = theta ** (-2.0 * jnp.arange(half, dtype=jnp.float32) / value_rows.shape[-1])
    angle = place[:, None, None] * freq
    cosine = jnp.cos(angle)
    sine_part = jnp.sin(angle)
    first = value_rows[..., :half]
    second = value_rows[..., half:]
    return jnp.concatenate(
        [first * cosine - second * sine_part, second * cosine + first * sine_part], axis=-1
    )


def request_place(order, lengths):
    ends = jnp.cumsum(lengths)
    starts = ends - lengths
    request = jnp.sum((order[:, None] >= ends[None, :]).astype(jnp.int32), axis=1)
    labels = jnp.arange(lengths.shape[0], dtype=jnp.int32)
    begin = jnp.sum(jnp.where(request[:, None] == labels[None, :], starts[None, :], 0), axis=1)
    return (request, order - begin)


from jax.experimental import pallas as pl
from jax.experimental.pallas import tpu as pltpu

TILE = 32
CHUNK = 256


def _attn_body(tables, q_ref, o_ref, rs_ref, req_ref, kv_ref, cache_ref, out_ref, *, group, scale):
    t = pl.program_id(0)
    rows = q_ref.shape[1]
    size = q_ref.shape[2]
    q = q_ref[...].reshape(group * rows, size)
    o_row = o_ref[...]
    rs_row = rs_ref[...]
    req_row = req_ref[...]

    def update(carry, keys, values, mask):
        top, total, accum = carry
        width = keys.shape[0]
        scores = lax.dot_general(q, keys, (((1,), (1,)), ((), ())), preferred_element_type=jnp.float32) * scale
        scores = scores.reshape(group, rows, width)
        scores = jnp.where(mask[None], scores, -1e30).reshape(group * rows, width)
        new_top = jnp.maximum(top, jnp.max(scores, axis=1, keepdims=True))
        expo = jnp.exp(scores - new_top).reshape(group, rows, width)
        expo = jnp.where(mask[None], expo, 0.0).reshape(group * rows, width)
        fade = jnp.exp(top - new_top)
        total = total * fade + jnp.sum(expo, axis=1, keepdims=True)
        accum = accum * fade + jnp.dot(expo.astype(jnp.bfloat16), values, preferred_element_type=jnp.float32)
        return (new_top, total, accum)

    def cached(r, carry):
        mask = req_row == r
        for j in range(2):
            block = cache_ref[2 * r + j]
            carry = update(carry, block[:, :size], block[:, size:], mask)
        return carry

    def fresh(c, carry):
        start = pl.multiple_of(c * CHUNK, CHUNK)
        block = kv_ref[pl.ds(start, CHUNK), :]
        index = start + lax.broadcasted_iota(jnp.int32, (1, CHUNK), 1)
        mask = (index >= rs_row) & (index <= o_row)
        return update(carry, block[:, :size], block[:, size:], mask)

    carry = (
        jnp.full((group * rows, 1), -1e30, jnp.float32),
        jnp.zeros((group * rows, 1), jnp.float32),
        jnp.zeros((group * rows, size), jnp.float32),
    )
    carry = lax.fori_loop(tables[0, t], tables[1, t] + 1, cached, carry)
    carry = lax.fori_loop(tables[2, t], tables[3, t] + 1, fresh, carry)
    top, total, accum = carry
    out_ref[...] = (accum / total).reshape(group, rows, size).astype(out_ref.dtype)


def sparse_attention(q_sorted, o_sorted, rs_sorted, req_sorted, kv_sorted, cache, interpret=False):
    group, count, size = q_sorted.shape
    tiles = count // TILE
    firsts = jnp.arange(tiles) * TILE
    lasts = firsts + TILE - 1
    tables = jnp.stack([
        req_sorted[firsts], req_sorted[lasts], rs_sorted[firsts] // CHUNK, o_sorted[lasts] // CHUNK
    ]).astype(jnp.int32)
    col = lambda v: v.reshape(count, 1).astype(jnp.int32)
    body = functools.partial(_attn_body, group=group, scale=size ** (-0.5))
    spec = pltpu.PrefetchScalarGridSpec(
        num_scalar_prefetch=1,
        grid=(tiles,),
        in_specs=[
            pl.BlockSpec((group, TILE, size), lambda t, tb: (0, t, 0)),
            pl.BlockSpec((TILE, 1), lambda t, tb: (t, 0)),
            pl.BlockSpec((TILE, 1), lambda t, tb: (t, 0)),
            pl.BlockSpec((TILE, 1), lambda t, tb: (t, 0)),
            pl.BlockSpec(kv_sorted.shape, lambda t, tb: (0, 0)),
            pl.BlockSpec(cache.shape, lambda t, tb: (0, 0, 0)),
        ],
        out_specs=pl.BlockSpec((group, TILE, size), lambda t, tb: (0, t, 0)),
    )
    return pl.pallas_call(
        body,
        grid_spec=spec,
        out_shape=jax.ShapeDtypeStruct(q_sorted.shape, jnp.bfloat16),
        compiler_params=pltpu.CompilerParams(dimension_semantics=("arbitrary",)),
        interpret=interpret,
    )(tables, q_sorted, col(o_sorted), col(rs_sorted), col(req_sorted), kv_sorted, cache)


def hand_over(arranged, device):
    parts = lax.psum(1, "seq")
    layers, slots = arranged.shape[0], arranged.shape[1]
    width = slots // parts
    chunks = arranged.reshape(layers, parts, width, *arranged.shape[2:])
    received = []
    for shift in range(parts):
        target = lax.rem(device + shift, parts)
        chunk = lax.dynamic_index_in_dim(chunks, target, 1, keepdims=False)
        if shift > 0:
            pairs = [(i, (i + shift) % parts) for i in range(parts)]
            chunk = lax.ppermute(chunk, "seq", pairs)
        received.append(chunk)
    stacked = jnp.stack(received, axis=2)
    sources = lax.rem(device - jnp.arange(parts, dtype=jnp.int32) + parts, parts)
    placed = jnp.take(stacked, sources, axis=2)
    return placed.reshape(layers, width, parts * arranged.shape[2], *arranged.shape[3:])


def gather_heads(piece):
    parts = lax.psum(1, "heads")
    me = lax.axis_index("heads")
    got = [piece]
    for shift in range(1, parts):
        pairs = [(i, (i + shift) % parts) for i in range(parts)]
        got.append(lax.ppermute(piece, "heads", pairs))
    stacked = jnp.stack(got, axis=0)
    stacked = jnp.take(stacked, lax.rem(me - jnp.arange(parts, dtype=jnp.int32) + parts, parts), axis=0)
    return jnp.transpose(stacked, (1, 0, 2)).reshape(piece.shape[0], parts * piece.shape[1])


def scatter_heads(partial_value):
    parts = lax.psum(1, "heads")
    me = lax.axis_index("heads")
    blocks = partial_value.reshape(partial_value.shape[0], parts, -1)
    total = lax.dynamic_index_in_dim(blocks, me, 1, keepdims=False)
    for shift in range(1, parts):
        pairs = [(i, (i + shift) % parts) for i in range(parts)]
        piece = lax.dynamic_index_in_dim(blocks, lax.rem(me + shift, parts), 1, keepdims=False)
        total = total + lax.ppermute(piece.astype(jnp.bfloat16), "heads", pairs).astype(jnp.float32)
    return total.astype(jnp.bfloat16)


def on_device(
    tokens,
    order,
    lengths,
    block_table,
    destination,
    w_query,
    key_weight,
    value_weight,
    w_out,
    key_value_cache,
):
    full = gather_heads(tokens)
    rows = full.shape[0]
    wide = full.astype(jnp.float32)
    normed = (wide * lax.rsqrt(jnp.mean(wide * wide, axis=1, keepdims=True) + epsilon)).astype(
        jnp.bfloat16
    )
    local_heads = key_weight.shape[1] // HEAD_SIZE
    head_group = QUERY_HEADS // KEY_VALUE_HEADS
    query_rows = jnp.dot(normed, w_query, preferred_element_type=jnp.float32)
    key_rows = jnp.dot(normed, key_weight, preferred_element_type=jnp.float32)
    value_rows = jnp.dot(normed, value_weight, preferred_element_type=jnp.float32)
    device = lax.axis_index("seq")
    my_order = lax.dynamic_slice_in_dim(order, device * rows, rows)
    request, position = request_place(my_order, lengths)
    rotary_angles = (position + CB * BLOCK_POSITIONS).astype(jnp.float32)
    query_rows = apply_rotary(
        query_rows.reshape(rows, local_heads * head_group, HEAD_SIZE), rotary_angles
    ).astype(jnp.bfloat16)
    query_rows = query_rows.reshape(rows, local_heads, head_group, HEAD_SIZE)
    key_rows = (
        apply_rotary(key_rows.reshape(rows, local_heads, HEAD_SIZE), rotary_angles)
        .astype(jnp.bfloat16)
        .reshape(rows, local_heads * HEAD_SIZE)
    )
    fresh_rows = jnp.concatenate(
        [
            key_rows.reshape(rows, local_heads, HEAD_SIZE),
            value_rows.astype(jnp.bfloat16).reshape(rows, local_heads, HEAD_SIZE),
        ],
        axis=2,
    ).reshape(rows, local_heads * 2 * HEAD_SIZE)
    gathered = lax.all_gather(fresh_rows, "seq", axis=0, tiled=True)
    kv_sorted = jnp.take(gathered, jnp.argsort(order), axis=0)
    layer_zero = key_value_cache[0]
    used = jnp.take(layer_zero, block_table.reshape(-1), axis=0)
    pool, span = used.shape[0], used.shape[1]
    used = used.reshape(pool, span, 2, local_heads, HEAD_SIZE).transpose(0, 1, 3, 2, 4)
    used = used.reshape(pool, span, local_heads * 2 * HEAD_SIZE)
    cache = lax.all_gather(used, "seq", axis=1, tiled=True)
    earlier = (my_order[None, :] < my_order[:, None]).astype(jnp.int32)
    unsort = jnp.sum(earlier, axis=1)
    slots_of = jnp.arange(rows, dtype=jnp.int32)
    perm = jnp.sum(jnp.where(unsort[:, None] == slots_of[None, :], slots_of[:, None], 0), axis=0)
    o_sorted = jnp.take(my_order, perm)
    rs_sorted = jnp.take(my_order - position, perm)
    req_sorted = jnp.take(request, perm)
    q_sorted = jnp.take(query_rows, perm, axis=0)
    outs = []
    for head in range(local_heads):
        result = sparse_attention(
            q_sorted[:, head].transpose(1, 0, 2),
            o_sorted,
            rs_sorted,
            req_sorted,
            kv_sorted[:, head * 2 * HEAD_SIZE:(head + 1) * 2 * HEAD_SIZE],
            cache[:, :, head * 2 * HEAD_SIZE:(head + 1) * 2 * HEAD_SIZE],
        )
        outs.append(jnp.take(result, unsort, axis=1).transpose(1, 0, 2))
    attn = jnp.stack(outs, axis=1).reshape(rows, local_heads * head_group * HEAD_SIZE)
    partial_value = jnp.dot(attn, w_out, preferred_element_type=jnp.float32)
    attn_out = scatter_heads(partial_value)
    slots = destination.shape[0]
    slot_labels = jnp.arange(slots, dtype=jnp.int32)
    inverse = jnp.sum(
        jnp.where(destination[None, :] == slot_labels[:, None], slot_labels[None, :], 0), axis=1
    )
    arranged = jnp.take(key_value_cache, inverse, axis=1)
    decode_cache = hand_over(arranged, device)
    return (attn_out, decode_cache)


def solution(mesh):
    placed = (
        P("seq", "heads"),
        P(),
        P(),
        P(),
        P(),
        P(None, "heads"),
        P(None, "heads"),
        P(None, "heads"),
        P("heads", None),
        P(None, None, "seq", None, "heads"),
    )
    return jax.shard_map(
        on_device,
        mesh=mesh,
        in_specs=placed,
        out_specs=(P("seq", "heads"), P(None, "seq", None, None, "heads")),
        check_vma=False,
    )
```

```python
import jax
import jax.numpy as jnp
from jax import lax
from jax.sharding import PartitionSpec as P
import functools
from jax.experimental import pallas as pl
from jax.experimental.pallas import tpu as pltpu

QUERY_HEADS = 40
KEY_VALUE_HEADS = 8
HEAD_SIZE = 128
BLOCK_POSITIONS = 512
CB = 2


theta = 1000000.0
epsilon = 1e-06


def apply_rotary(value_rows, place):
    half = value_rows.shape[-1] // 2
    freq = theta ** (-2.0 * jnp.arange(half, dtype=jnp.float32) / value_rows.shape[-1])
    angle = place[:, None, None] * freq
    cosine = jnp.cos(angle)
    sine_part = jnp.sin(angle)
    first = value_rows[..., :half]
    second = value_rows[..., half:]
    return jnp.concatenate(
        [first * cosine - second * sine_part, second * cosine + first * sine_part], axis=-1
    )


def request_place(order, lengths):
    ends = jnp.cumsum(lengths)
    starts = ends - lengths
    request = jnp.sum((order[:, None] >= ends[None, :]).astype(jnp.int32), axis=1)
    labels = jnp.arange(lengths.shape[0], dtype=jnp.int32)
    begin = jnp.sum(jnp.where(request[:, None] == labels[None, :], starts[None, :], 0), axis=1)
    return (request, order - begin)


from jax.experimental import pallas as pl
from jax.experimental.pallas import tpu as pltpu

TILE = 32
CHUNK = 256


def _attn_body(tables, q_ref, o_ref, rs_ref, req_ref, kv_ref, cache_ref, out_ref, *, group, scale):
    t = pl.program_id(0)
    rows = q_ref.shape[1]
    size = q_ref.shape[2]
    q = q_ref[...].reshape(group * rows, size)
    o_row = o_ref[...]
    rs_row = rs_ref[...]
    req_row = req_ref[...]

    def update(carry, keys, values, mask):
        top, total, accum = carry
        width = keys.shape[0]
        scores = lax.dot_general(q, keys, (((1,), (1,)), ((), ())), preferred_element_type=jnp.float32) * scale
        scores = scores.reshape(group, rows, width)
        scores = jnp.where(mask[None], scores, -1e30).reshape(group * rows, width)
        new_top = jnp.maximum(top, jnp.max(scores, axis=1, keepdims=True))
        expo = jnp.exp(scores - new_top).reshape(group, rows, width)
        expo = jnp.where(mask[None], expo, 0.0).reshape(group * rows, width)
        fade = jnp.exp(top - new_top)
        total = total * fade + jnp.sum(expo, axis=1, keepdims=True)
        accum = accum * fade + jnp.dot(expo.astype(jnp.bfloat16), values, preferred_element_type=jnp.float32)
        return (new_top, total, accum)

    def cached(r, carry):
        mask = req_row == r
        for j in range(2):
            block = cache_ref[2 * r + j]
            carry = update(carry, block[:, :size], block[:, size:], mask)
        return carry

    def fresh(c, carry):
        start = pl.multiple_of(c * CHUNK, CHUNK)
        block = kv_ref[pl.ds(start, CHUNK), :]
        index = start + lax.broadcasted_iota(jnp.int32, (1, CHUNK), 1)
        mask = (index >= rs_row) & (index <= o_row)
        return update(carry, block[:, :size], block[:, size:], mask)

    carry = (
        jnp.full((group * rows, 1), -1e30, jnp.float32),
        jnp.zeros((group * rows, 1), jnp.float32),
        jnp.zeros((group * rows, size), jnp.float32),
    )
    carry = lax.fori_loop(tables[0, t], tables[1, t] + 1, cached, carry)
    carry = lax.fori_loop(tables[2, t], tables[3, t] + 1, fresh, carry)
    top, total, accum = carry
    out_ref[...] = (accum / total).reshape(group, rows, size).astype(out_ref.dtype)


def sparse_attention(q_sorted, o_sorted, rs_sorted, req_sorted, kv_sorted, cache, interpret=False):
    group, count, size = q_sorted.shape
    tiles = count // TILE
    firsts = jnp.arange(tiles) * TILE
    lasts = firsts + TILE - 1
    tables = jnp.stack([
        req_sorted[firsts], req_sorted[lasts], rs_sorted[firsts] // CHUNK, o_sorted[lasts] // CHUNK
    ]).astype(jnp.int32)
    col = lambda v: v.reshape(count, 1).astype(jnp.int32)
    body = functools.partial(_attn_body, group=group, scale=size ** (-0.5))
    spec = pltpu.PrefetchScalarGridSpec(
        num_scalar_prefetch=1,
        grid=(tiles,),
        in_specs=[
            pl.BlockSpec((group, TILE, size), lambda t, tb: (0, t, 0)),
            pl.BlockSpec((TILE, 1), lambda t, tb: (t, 0)),
            pl.BlockSpec((TILE, 1), lambda t, tb: (t, 0)),
            pl.BlockSpec((TILE, 1), lambda t, tb: (t, 0)),
            pl.BlockSpec(kv_sorted.shape, lambda t, tb: (0, 0)),
            pl.BlockSpec(cache.shape, lambda t, tb: (0, 0, 0)),
        ],
        out_specs=pl.BlockSpec((group, TILE, size), lambda t, tb: (0, t, 0)),
    )
    return pl.pallas_call(
        body,
        grid_spec=spec,
        out_shape=jax.ShapeDtypeStruct(q_sorted.shape, jnp.bfloat16),
        compiler_params=pltpu.CompilerParams(dimension_semantics=("arbitrary",)),
        interpret=interpret,
    )(tables, q_sorted, col(o_sorted), col(rs_sorted), col(req_sorted), kv_sorted, cache)


def rotate_columns(value, shift):
    doubled = jnp.concatenate([value, value], axis=1)
    return lax.dynamic_slice_in_dim(doubled, shift, value.shape[1], axis=1)


def gather_heads(piece):
    parts = lax.psum(1, "heads")
    me = lax.axis_index("heads")
    got = {0: piece}
    for shift in range(1, parts):
        pairs = [(i, (i + shift) % parts) for i in range(parts)]
        got[shift] = lax.ppermute(piece, "heads", pairs)
    ahead = jnp.concatenate([got[(parts - j) % parts] for j in range(parts)], axis=1)
    width = piece.shape[1]
    return rotate_columns(ahead, (parts - me) % parts * width)


def scatter_heads(partial_value):
    parts = lax.psum(1, "heads")
    me = lax.axis_index("heads")
    width = partial_value.shape[1] // parts
    ahead = rotate_columns(partial_value.astype(jnp.bfloat16), me * width)
    total = ahead[:, :width].astype(jnp.float32)
    for shift in range(1, parts):
        pairs = [(i, (i + shift) % parts) for i in range(parts)]
        piece = ahead[:, shift * width:(shift + 1) * width]
        total = total + lax.ppermute(piece, "heads", pairs).astype(jnp.float32)
    return total.astype(jnp.bfloat16)


def on_device(
    tokens,
    order,
    lengths,
    block_table,
    destination,
    w_query,
    key_weight,
    value_weight,
    w_out,
    key_value_cache,
):
    slots = destination.shape[0]
    slot_labels = jnp.arange(slots, dtype=jnp.int32)
    inverse = jnp.sum(
        jnp.where(destination[None, :] == slot_labels[:, None], slot_labels[None, :], 0), axis=1
    )
    arranged = jnp.take(key_value_cache, inverse, axis=1)
    decode_cache = lax.all_to_all(arranged, "seq", split_axis=1, concat_axis=2, tiled=True)
    full, decode_cache = lax.optimization_barrier((gather_heads(tokens), decode_cache))
    rows = full.shape[0]
    wide = full.astype(jnp.float32)
    normed = (wide * lax.rsqrt(jnp.mean(wide * wide, axis=1, keepdims=True) + epsilon)).astype(
        jnp.bfloat16
    )
    local_heads = key_weight.shape[1] // HEAD_SIZE
    head_group = QUERY_HEADS // KEY_VALUE_HEADS
    query_rows = jnp.dot(normed, w_query, preferred_element_type=jnp.float32)
    key_rows = jnp.dot(normed, key_weight, preferred_element_type=jnp.float32)
    value_rows = jnp.dot(normed, value_weight, preferred_element_type=jnp.float32)
    device = lax.axis_index("seq")
    my_order = lax.dynamic_slice_in_dim(order, device * rows, rows)
    request, position = request_place(my_order, lengths)
    rotary_angles = (position + CB * BLOCK_POSITIONS).astype(jnp.float32)
    query_rows = apply_rotary(
        query_rows.reshape(rows, local_heads * head_group, HEAD_SIZE), rotary_angles
    ).astype(jnp.bfloat16)
    query_rows = query_rows.reshape(rows, local_heads, head_group, HEAD_SIZE)
    key_rows = (
        apply_rotary(key_rows.reshape(rows, local_heads, HEAD_SIZE), rotary_angles)
        .astype(jnp.bfloat16)
        .reshape(rows, local_heads * HEAD_SIZE)
    )
    fresh_rows = jnp.concatenate(
        [
            key_rows.reshape(rows, local_heads, HEAD_SIZE),
            value_rows.astype(jnp.bfloat16).reshape(rows, local_heads, HEAD_SIZE),
        ],
        axis=2,
    ).reshape(rows, local_heads * 2 * HEAD_SIZE)
    gathered = lax.all_gather(fresh_rows, "seq", axis=0, tiled=True)
    kv_sorted = jnp.take(gathered, jnp.argsort(order), axis=0)
    layer_zero = key_value_cache[0]
    used = jnp.take(layer_zero, block_table.reshape(-1), axis=0)
    pool, span = used.shape[0], used.shape[1]
    used = used.reshape(pool, span, 2, local_heads, HEAD_SIZE).transpose(0, 1, 3, 2, 4)
    used = used.reshape(pool, span, local_heads * 2 * HEAD_SIZE)
    cache = lax.all_gather(used, "seq", axis=1, tiled=True)
    earlier = (my_order[None, :] < my_order[:, None]).astype(jnp.int32)
    unsort = jnp.sum(earlier, axis=1)
    slots_of = jnp.arange(rows, dtype=jnp.int32)
    perm = jnp.sum(jnp.where(unsort[:, None] == slots_of[None, :], slots_of[:, None], 0), axis=0)
    o_sorted = jnp.take(my_order, perm)
    rs_sorted = jnp.take(my_order - position, perm)
    req_sorted = jnp.take(request, perm)
    q_sorted = jnp.take(query_rows, perm, axis=0)
    outs = []
    for head in range(local_heads):
        result = sparse_attention(
            q_sorted[:, head].transpose(1, 0, 2),
            o_sorted,
            rs_sorted,
            req_sorted,
            kv_sorted[:, head * 2 * HEAD_SIZE:(head + 1) * 2 * HEAD_SIZE],
            cache[:, :, head * 2 * HEAD_SIZE:(head + 1) * 2 * HEAD_SIZE],
        )
        outs.append(jnp.take(result, unsort, axis=1).transpose(1, 0, 2))
    attn = jnp.stack(outs, axis=1).reshape(rows, local_heads * head_group * HEAD_SIZE)
    partial_value = jnp.dot(attn, w_out, preferred_element_type=jnp.float32)
    attn_out = scatter_heads(partial_value)
    return (attn_out, decode_cache)


def solution(mesh):
    placed = (
        P("seq", "heads"),
        P(),
        P(),
        P(),
        P(),
        P(None, "heads"),
        P(None, "heads"),
        P(None, "heads"),
        P("heads", None),
        P(None, None, "seq", None, "heads"),
    )
    return jax.shard_map(
        on_device,
        mesh=mesh,
        in_specs=placed,
        out_specs=(P("seq", "heads"), P(None, "seq", None, None, "heads")),
        check_vma=False,
    )
```

```python
import jax
import jax.numpy as jnp
from jax import lax
from jax.sharding import PartitionSpec as P
import functools
from jax.experimental import pallas as pl
from jax.experimental.pallas import tpu as pltpu

QUERY_HEADS = 40
KEY_VALUE_HEADS = 8
HEAD_SIZE = 128
BLOCK_POSITIONS = 512
CB = 2


theta = 1000000.0
epsilon = 1e-06


def apply_rotary(value_rows, place):
    half = value_rows.shape[-1] // 2
    freq = theta ** (-2.0 * jnp.arange(half, dtype=jnp.float32) / value_rows.shape[-1])
    angle = place[:, None, None] * freq
    cosine = jnp.cos(angle)
    sine_part = jnp.sin(angle)
    first = value_rows[..., :half]
    second = value_rows[..., half:]
    return jnp.concatenate(
        [first * cosine - second * sine_part, second * cosine + first * sine_part], axis=-1
    )


def request_place(order, lengths):
    ends = jnp.cumsum(lengths)
    starts = ends - lengths
    request = jnp.sum((order[:, None] >= ends[None, :]).astype(jnp.int32), axis=1)
    labels = jnp.arange(lengths.shape[0], dtype=jnp.int32)
    begin = jnp.sum(jnp.where(request[:, None] == labels[None, :], starts[None, :], 0), axis=1)
    return (request, order - begin)


from jax.experimental import pallas as pl
from jax.experimental.pallas import tpu as pltpu

TILE = 32
CHUNK = 256


def _online(q, keys, values, mask, carry, scale):
    top, total, accum = carry
    width = keys.shape[0]
    scores = lax.dot_general(q, keys, (((1,), (1,)), ((), ())), preferred_element_type=jnp.float32) * scale
    scores = scores.reshape(-1, mask.shape[0], width)
    scores = jnp.where(mask[None], scores, -1e30).reshape(q.shape[0], width)
    new_top = jnp.maximum(top, jnp.max(scores, axis=1, keepdims=True))
    expo = jnp.exp(scores - new_top).reshape(-1, mask.shape[0], width)
    expo = jnp.where(mask[None], expo, 0.0).reshape(q.shape[0], width)
    fade = jnp.exp(top - new_top)
    total = total * fade + jnp.sum(expo, axis=1, keepdims=True)
    accum = accum * fade + jnp.dot(expo.astype(jnp.bfloat16), values, preferred_element_type=jnp.float32)
    return (new_top, total, accum)


def _cache_body(tables, q_ref, req_ref, cache_ref, top_ref, total_ref, accum_ref, *, scale):
    t = pl.program_id(0)
    group, rows, size = q_ref.shape
    q = q_ref[...].reshape(group * rows, size)
    req_row = req_ref[...]

    def cached(r, carry):
        mask = req_row == r
        for j in range(2):
            block = cache_ref[2 * r + j]
            carry = _online(q, block[:, :size], block[:, size:], mask, carry, scale)
        return carry

    carry = (
        jnp.full((group * rows, 1), -1e30, jnp.float32),
        jnp.zeros((group * rows, 1), jnp.float32),
        jnp.zeros((group * rows, size), jnp.float32),
    )
    top, total, accum = lax.fori_loop(tables[0, t], tables[1, t] + 1, cached, carry)
    top_ref[...] = top
    total_ref[...] = total
    accum_ref[...] = accum


def _fresh_body(tables, q_ref, o_ref, rs_ref, top_ref, total_ref, accum_ref, kv_ref, out_ref, *, scale):
    t = pl.program_id(0)
    group, rows, size = q_ref.shape
    q = q_ref[...].reshape(group * rows, size)
    o_row = o_ref[...]
    rs_row = rs_ref[...]

    def fresh(c, carry):
        start = pl.multiple_of(c * CHUNK, CHUNK)
        block = kv_ref[pl.ds(start, CHUNK), :]
        index = start + lax.broadcasted_iota(jnp.int32, (1, CHUNK), 1)
        mask = (index >= rs_row) & (index <= o_row)
        return _online(q, block[:, :size], block[:, size:], mask, carry, scale)

    carry = (top_ref[...], total_ref[...], accum_ref[...])
    top, total, accum = lax.fori_loop(tables[2, t], tables[3, t] + 1, fresh, carry)
    out_ref[...] = (accum / total).reshape(group, rows, size).astype(out_ref.dtype)


def attention_tables(o_sorted, rs_sorted, req_sorted):
    count = o_sorted.shape[0]
    firsts = jnp.arange(count // TILE) * TILE
    lasts = firsts + TILE - 1
    return jnp.stack([
        req_sorted[firsts], req_sorted[lasts], rs_sorted[firsts] // CHUNK, o_sorted[lasts] // CHUNK
    ]).astype(jnp.int32)


def cache_attention(tables, q_sorted, req_sorted, cache):
    group, count, size = q_sorted.shape
    tiles = count // TILE
    body = functools.partial(_cache_body, scale=size ** (-0.5))
    state = pl.BlockSpec((group * TILE, 1), lambda t, tb: (t, 0))
    spec = pltpu.PrefetchScalarGridSpec(
        num_scalar_prefetch=1,
        grid=(tiles,),
        in_specs=[
            pl.BlockSpec((group, TILE, size), lambda t, tb: (0, t, 0)),
            pl.BlockSpec((TILE, 1), lambda t, tb: (t, 0)),
            pl.BlockSpec(cache.shape, lambda t, tb: (0, 0, 0)),
        ],
        out_specs=[state, state, pl.BlockSpec((group * TILE, size), lambda t, tb: (t, 0))],
    )
    return pl.pallas_call(
        body,
        grid_spec=spec,
        out_shape=[
            jax.ShapeDtypeStruct((group * count, 1), jnp.float32),
            jax.ShapeDtypeStruct((group * count, 1), jnp.float32),
            jax.ShapeDtypeStruct((group * count, size), jnp.float32),
        ],
        compiler_params=pltpu.CompilerParams(dimension_semantics=("arbitrary",)),
    )(tables, q_sorted, req_sorted.reshape(count, 1), cache)


def fresh_attention(tables, q_sorted, o_sorted, rs_sorted, state, kv_sorted):
    group, count, size = q_sorted.shape
    tiles = count // TILE
    body = functools.partial(_fresh_body, scale=size ** (-0.5))
    column = pl.BlockSpec((TILE, 1), lambda t, tb: (t, 0))
    lane = pl.BlockSpec((group * TILE, 1), lambda t, tb: (t, 0))
    spec = pltpu.PrefetchScalarGridSpec(
        num_scalar_prefetch=1,
        grid=(tiles,),
        in_specs=[
            pl.BlockSpec((group, TILE, size), lambda t, tb: (0, t, 0)),
            column,
            column,
            lane,
            lane,
            pl.BlockSpec((group * TILE, size), lambda t, tb: (t, 0)),
            pl.BlockSpec(kv_sorted.shape, lambda t, tb: (0, 0)),
        ],
        out_specs=pl.BlockSpec((group, TILE, size), lambda t, tb: (0, t, 0)),
    )
    return pl.pallas_call(
        body,
        grid_spec=spec,
        out_shape=jax.ShapeDtypeStruct(q_sorted.shape, jnp.bfloat16),
        compiler_params=pltpu.CompilerParams(dimension_semantics=("arbitrary",)),
    )(tables, q_sorted, o_sorted.reshape(count, 1), rs_sorted.reshape(count, 1), *state, kv_sorted)


def rotate_columns(value, shift):
    doubled = jnp.concatenate([value, value], axis=1)
    return lax.dynamic_slice_in_dim(doubled, shift, value.shape[1], axis=1)


def gather_heads(piece):
    parts = lax.psum(1, "heads")
    me = lax.axis_index("heads")
    got = {0: piece}
    for shift in range(1, parts):
        pairs = [(i, (i + shift) % parts) for i in range(parts)]
        got[shift] = lax.ppermute(piece, "heads", pairs)
    ahead = jnp.concatenate([got[(parts - j) % parts] for j in range(parts)], axis=1)
    width = piece.shape[1]
    return rotate_columns(ahead, (parts - me) % parts * width)


def scatter_heads(partial_value):
    parts = lax.psum(1, "heads")
    me = lax.axis_index("heads")
    width = partial_value.shape[1] // parts
    ahead = rotate_columns(partial_value.astype(jnp.bfloat16), me * width)
    total = ahead[:, :width].astype(jnp.float32)
    for shift in range(1, parts):
        pairs = [(i, (i + shift) % parts) for i in range(parts)]
        piece = ahead[:, shift * width:(shift + 1) * width]
        total = total + lax.ppermute(piece, "heads", pairs).astype(jnp.float32)
    return total.astype(jnp.bfloat16)


def on_device(
    tokens,
    order,
    lengths,
    block_table,
    destination,
    w_query,
    key_weight,
    value_weight,
    w_out,
    key_value_cache,
):
    slots = destination.shape[0]
    slot_labels = jnp.arange(slots, dtype=jnp.int32)
    inverse = jnp.sum(
        jnp.where(destination[None, :] == slot_labels[:, None], slot_labels[None, :], 0), axis=1
    )
    arranged = jnp.take(key_value_cache, inverse, axis=1)
    full, arranged = lax.optimization_barrier((gather_heads(tokens), arranged))
    rows = full.shape[0]
    wide = full.astype(jnp.float32)
    normed = (wide * lax.rsqrt(jnp.mean(wide * wide, axis=1, keepdims=True) + epsilon)).astype(
        jnp.bfloat16
    )
    local_heads = key_weight.shape[1] // HEAD_SIZE
    head_group = QUERY_HEADS // KEY_VALUE_HEADS
    query_rows = jnp.dot(normed, w_query, preferred_element_type=jnp.float32)
    key_rows = jnp.dot(normed, key_weight, preferred_element_type=jnp.float32)
    value_rows = jnp.dot(normed, value_weight, preferred_element_type=jnp.float32)
    device = lax.axis_index("seq")
    my_order = lax.dynamic_slice_in_dim(order, device * rows, rows)
    request, position = request_place(my_order, lengths)
    rotary_angles = (position + CB * BLOCK_POSITIONS).astype(jnp.float32)
    query_rows = apply_rotary(
        query_rows.reshape(rows, local_heads * head_group, HEAD_SIZE), rotary_angles
    ).astype(jnp.bfloat16)
    query_rows = query_rows.reshape(rows, local_heads, head_group, HEAD_SIZE)
    key_rows = (
        apply_rotary(key_rows.reshape(rows, local_heads, HEAD_SIZE), rotary_angles)
        .astype(jnp.bfloat16)
        .reshape(rows, local_heads * HEAD_SIZE)
    )
    fresh_rows = jnp.concatenate(
        [
            key_rows.reshape(rows, local_heads, HEAD_SIZE),
            value_rows.astype(jnp.bfloat16).reshape(rows, local_heads, HEAD_SIZE),
        ],
        axis=2,
    ).reshape(rows, local_heads * 2 * HEAD_SIZE)
    gathered = lax.all_gather(fresh_rows, "seq", axis=0, tiled=True)
    kv_sorted = jnp.take(gathered, jnp.argsort(order), axis=0)
    layer_zero = key_value_cache[0]
    used = jnp.take(layer_zero, block_table.reshape(-1), axis=0)
    pool, span = used.shape[0], used.shape[1]
    used = used.reshape(pool, span, 2, local_heads, HEAD_SIZE).transpose(0, 1, 3, 2, 4)
    used = used.reshape(pool, span, local_heads * 2 * HEAD_SIZE)
    cache = lax.all_gather(used, "seq", axis=1, tiled=True)
    earlier = (my_order[None, :] < my_order[:, None]).astype(jnp.int32)
    unsort = jnp.sum(earlier, axis=1)
    slots_of = jnp.arange(rows, dtype=jnp.int32)
    perm = jnp.sum(jnp.where(unsort[:, None] == slots_of[None, :], slots_of[:, None], 0), axis=0)
    o_sorted = jnp.take(my_order, perm)
    rs_sorted = jnp.take(my_order - position, perm)
    req_sorted = jnp.take(request, perm)
    q_sorted = jnp.take(query_rows, perm, axis=0)
    tables = attention_tables(o_sorted, rs_sorted, req_sorted)
    q_sorted, arranged = lax.optimization_barrier((q_sorted, arranged))
    decode_cache = lax.all_to_all(arranged, "seq", split_axis=1, concat_axis=2, tiled=True)
    outs = []
    for head in range(local_heads):
        q_head = q_sorted[:, head].transpose(1, 0, 2)
        part = slice(head * 2 * HEAD_SIZE, (head + 1) * 2 * HEAD_SIZE)
        state = cache_attention(tables, q_head, req_sorted, cache[:, :, part])
        result = fresh_attention(tables, q_head, o_sorted, rs_sorted, state, kv_sorted[:, part])
        outs.append(result)
    outs, decode_cache = lax.optimization_barrier((outs, decode_cache))
    outs = [jnp.take(result, unsort, axis=1).transpose(1, 0, 2) for result in outs]
    attn = jnp.stack(outs, axis=1).reshape(rows, local_heads * head_group * HEAD_SIZE)
    partial_value = jnp.dot(attn, w_out, preferred_element_type=jnp.float32)
    attn_out = scatter_heads(partial_value)
    return (attn_out, decode_cache)


def solution(mesh):
    placed = (
        P("seq", "heads"),
        P(),
        P(),
        P(),
        P(),
        P(None, "heads"),
        P(None, "heads"),
        P(None, "heads"),
        P("heads", None),
        P(None, None, "seq", None, "heads"),
    )
    return jax.shard_map(
        on_device,
        mesh=mesh,
        in_specs=placed,
        out_specs=(P("seq", "heads"), P(None, "seq", None, None, "heads")),
        check_vma=False,
    )
```

```python
import jax
import jax.numpy as jnp
from jax import lax
from jax.sharding import PartitionSpec as P
import functools
from jax.experimental import pallas as pl
from jax.experimental.pallas import tpu as pltpu

QUERY_HEADS = 40
KEY_VALUE_HEADS = 8
HEAD_SIZE = 128
BLOCK_POSITIONS = 512
CB = 2


theta = 1000000.0
epsilon = 1e-06


def apply_rotary(value_rows, place):
    half = value_rows.shape[-1] // 2
    freq = theta ** (-2.0 * jnp.arange(half, dtype=jnp.float32) / value_rows.shape[-1])
    angle = place[:, None, None] * freq
    cosine = jnp.cos(angle)
    sine_part = jnp.sin(angle)
    first = value_rows[..., :half]
    second = value_rows[..., half:]
    return jnp.concatenate(
        [first * cosine - second * sine_part, second * cosine + first * sine_part], axis=-1
    )


def request_place(order, lengths):
    ends = jnp.cumsum(lengths)
    starts = ends - lengths
    request = jnp.sum((order[:, None] >= ends[None, :]).astype(jnp.int32), axis=1)
    labels = jnp.arange(lengths.shape[0], dtype=jnp.int32)
    begin = jnp.sum(jnp.where(request[:, None] == labels[None, :], starts[None, :], 0), axis=1)
    return (request, order - begin)


from jax.experimental import pallas as pl
from jax.experimental.pallas import tpu as pltpu

TILE = 32
CHUNK = 256


def _online(q, keys, values, mask, carry, scale):
    top, total, accum = carry
    width = keys.shape[0]
    scores = lax.dot_general(q, keys, (((1,), (1,)), ((), ())), preferred_element_type=jnp.float32) * scale
    scores = scores.reshape(-1, mask.shape[0], width)
    scores = jnp.where(mask[None], scores, -1e30).reshape(q.shape[0], width)
    new_top = jnp.maximum(top, jnp.max(scores, axis=1, keepdims=True))
    expo = jnp.exp(scores - new_top).reshape(-1, mask.shape[0], width)
    expo = jnp.where(mask[None], expo, 0.0).reshape(q.shape[0], width)
    fade = jnp.exp(top - new_top)
    total = total * fade + jnp.sum(expo, axis=1, keepdims=True)
    accum = accum * fade + jnp.dot(expo.astype(jnp.bfloat16), values, preferred_element_type=jnp.float32)
    return (new_top, total, accum)


def _cache_body(tables, q_ref, req_ref, cache_ref, top_ref, total_ref, accum_ref, *, scale):
    t = pl.program_id(0)
    group, rows, size = q_ref.shape
    q = q_ref[...].reshape(group * rows, size)
    req_row = req_ref[...]

    def cached(r, carry):
        mask = req_row == r
        for j in range(2):
            block = cache_ref[2 * r + j]
            carry = _online(q, block[:, :size], block[:, size:], mask, carry, scale)
        return carry

    carry = (
        jnp.full((group * rows, 1), -1e30, jnp.float32),
        jnp.zeros((group * rows, 1), jnp.float32),
        jnp.zeros((group * rows, size), jnp.float32),
    )
    top, total, accum = lax.fori_loop(tables[0, t], tables[1, t] + 1, cached, carry)
    top_ref[...] = top
    total_ref[...] = total
    accum_ref[...] = accum


def _fresh_body(tables, q_ref, o_ref, rs_ref, top_ref, total_ref, accum_ref, kv_ref, out_ref, *, scale):
    t = pl.program_id(0)
    group, rows, size = q_ref.shape
    q = q_ref[...].reshape(group * rows, size)
    o_row = o_ref[...]
    rs_row = rs_ref[...]

    def fresh(c, carry):
        start = pl.multiple_of(c * CHUNK, CHUNK)
        block = kv_ref[pl.ds(start, CHUNK), :]
        index = start + lax.broadcasted_iota(jnp.int32, (1, CHUNK), 1)
        mask = (index >= rs_row) & (index <= o_row)
        return _online(q, block[:, :size], block[:, size:], mask, carry, scale)

    carry = (top_ref[...], total_ref[...], accum_ref[...])
    top, total, accum = lax.fori_loop(tables[2, t], tables[3, t] + 1, fresh, carry)
    out_ref[...] = (accum / total).reshape(group, rows, size).astype(out_ref.dtype)


def attention_tables(o_sorted, rs_sorted, req_sorted):
    count = o_sorted.shape[0]
    firsts = jnp.arange(count // TILE) * TILE
    lasts = firsts + TILE - 1
    return jnp.stack([
        req_sorted[firsts], req_sorted[lasts], rs_sorted[firsts] // CHUNK, o_sorted[lasts] // CHUNK
    ]).astype(jnp.int32)


def cache_attention(tables, q_sorted, req_sorted, cache):
    group, count, size = q_sorted.shape
    tiles = count // TILE
    body = functools.partial(_cache_body, scale=size ** (-0.5))
    state = pl.BlockSpec((group * TILE, 1), lambda t, tb: (t, 0))
    spec = pltpu.PrefetchScalarGridSpec(
        num_scalar_prefetch=1,
        grid=(tiles,),
        in_specs=[
            pl.BlockSpec((group, TILE, size), lambda t, tb: (0, t, 0)),
            pl.BlockSpec((TILE, 1), lambda t, tb: (t, 0)),
            pl.BlockSpec(cache.shape, lambda t, tb: (0, 0, 0)),
        ],
        out_specs=[state, state, pl.BlockSpec((group * TILE, size), lambda t, tb: (t, 0))],
    )
    return pl.pallas_call(
        body,
        grid_spec=spec,
        out_shape=[
            jax.ShapeDtypeStruct((group * count, 1), jnp.float32),
            jax.ShapeDtypeStruct((group * count, 1), jnp.float32),
            jax.ShapeDtypeStruct((group * count, size), jnp.float32),
        ],
        compiler_params=pltpu.CompilerParams(dimension_semantics=("arbitrary",)),
    )(tables, q_sorted, req_sorted.reshape(count, 1), cache)


def fresh_attention(tables, q_sorted, o_sorted, rs_sorted, state, kv_sorted):
    group, count, size = q_sorted.shape
    tiles = count // TILE
    body = functools.partial(_fresh_body, scale=size ** (-0.5))
    column = pl.BlockSpec((TILE, 1), lambda t, tb: (t, 0))
    lane = pl.BlockSpec((group * TILE, 1), lambda t, tb: (t, 0))
    spec = pltpu.PrefetchScalarGridSpec(
        num_scalar_prefetch=1,
        grid=(tiles,),
        in_specs=[
            pl.BlockSpec((group, TILE, size), lambda t, tb: (0, t, 0)),
            column,
            column,
            lane,
            lane,
            pl.BlockSpec((group * TILE, size), lambda t, tb: (t, 0)),
            pl.BlockSpec(kv_sorted.shape, lambda t, tb: (0, 0)),
        ],
        out_specs=pl.BlockSpec((group, TILE, size), lambda t, tb: (0, t, 0)),
    )
    return pl.pallas_call(
        body,
        grid_spec=spec,
        out_shape=jax.ShapeDtypeStruct(q_sorted.shape, jnp.bfloat16),
        compiler_params=pltpu.CompilerParams(dimension_semantics=("arbitrary",)),
    )(tables, q_sorted, o_sorted.reshape(count, 1), rs_sorted.reshape(count, 1), *state, kv_sorted)


def rotate_columns(value, shift):
    doubled = jnp.concatenate([value, value], axis=1)
    return lax.dynamic_slice_in_dim(doubled, shift, value.shape[1], axis=1)


def gather_heads(piece):
    parts = lax.psum(1, "heads")
    me = lax.axis_index("heads")
    got = {0: piece}
    for shift in range(1, parts):
        pairs = [(i, (i + shift) % parts) for i in range(parts)]
        got[shift] = lax.ppermute(piece, "heads", pairs)
    ahead = jnp.concatenate([got[(parts - j) % parts] for j in range(parts)], axis=1)
    width = piece.shape[1]
    return rotate_columns(ahead, (parts - me) % parts * width)


def scatter_heads(partial_value):
    parts = lax.psum(1, "heads")
    me = lax.axis_index("heads")
    width = partial_value.shape[1] // parts
    ahead = rotate_columns(partial_value.astype(jnp.bfloat16), me * width)
    total = ahead[:, :width].astype(jnp.float32)
    for shift in range(1, parts):
        pairs = [(i, (i + shift) % parts) for i in range(parts)]
        piece = ahead[:, shift * width:(shift + 1) * width]
        total = total + lax.ppermute(piece, "heads", pairs).astype(jnp.float32)
    return total.astype(jnp.bfloat16)


def on_device(
    tokens,
    order,
    lengths,
    block_table,
    destination,
    w_query,
    key_weight,
    value_weight,
    w_out,
    key_value_cache,
):
    local_heads = key_weight.shape[1] // HEAD_SIZE
    slots = destination.shape[0]
    slot_labels = jnp.arange(slots, dtype=jnp.int32)
    inverse = jnp.sum(
        jnp.where(destination[None, :] == slot_labels[:, None], slot_labels[None, :], 0), axis=1
    )
    arranged = jnp.take(key_value_cache, inverse, axis=1)
    layer_zero = key_value_cache[0]
    used = jnp.take(layer_zero, block_table.reshape(-1), axis=0)
    pool, span = used.shape[0], used.shape[1]
    used = used.reshape(pool, span, 2, local_heads, HEAD_SIZE).transpose(0, 1, 3, 2, 4)
    used = used.reshape(pool, span, local_heads * 2 * HEAD_SIZE)
    cache = lax.all_gather(used, "seq", axis=1, tiled=True)
    by_order = jnp.argsort(order)
    full, arranged, cache, by_order = lax.optimization_barrier((gather_heads(tokens), arranged, cache, by_order))
    rows = full.shape[0]
    wide = full.astype(jnp.float32)
    normed = (wide * lax.rsqrt(jnp.mean(wide * wide, axis=1, keepdims=True) + epsilon)).astype(
        jnp.bfloat16
    )
    local_heads = key_weight.shape[1] // HEAD_SIZE
    head_group = QUERY_HEADS // KEY_VALUE_HEADS
    query_rows = jnp.dot(normed, w_query, preferred_element_type=jnp.float32)
    key_rows = jnp.dot(normed, key_weight, preferred_element_type=jnp.float32)
    value_rows = jnp.dot(normed, value_weight, preferred_element_type=jnp.float32)
    device = lax.axis_index("seq")
    my_order = lax.dynamic_slice_in_dim(order, device * rows, rows)
    request, position = request_place(my_order, lengths)
    rotary_angles = (position + CB * BLOCK_POSITIONS).astype(jnp.float32)
    query_rows = apply_rotary(
        query_rows.reshape(rows, local_heads * head_group, HEAD_SIZE), rotary_angles
    ).astype(jnp.bfloat16)
    query_rows = query_rows.reshape(rows, local_heads, head_group, HEAD_SIZE)
    key_rows = (
        apply_rotary(key_rows.reshape(rows, local_heads, HEAD_SIZE), rotary_angles)
        .astype(jnp.bfloat16)
        .reshape(rows, local_heads * HEAD_SIZE)
    )
    fresh_rows = jnp.concatenate(
        [
            key_rows.reshape(rows, local_heads, HEAD_SIZE),
            value_rows.astype(jnp.bfloat16).reshape(rows, local_heads, HEAD_SIZE),
        ],
        axis=2,
    ).reshape(rows, local_heads * 2 * HEAD_SIZE)
    gathered = lax.all_gather(fresh_rows, "seq", axis=0, tiled=True)
    kv_sorted = jnp.take(gathered, by_order, axis=0)
    earlier = (my_order[None, :] < my_order[:, None]).astype(jnp.int32)
    unsort = jnp.sum(earlier, axis=1)
    slots_of = jnp.arange(rows, dtype=jnp.int32)
    perm = jnp.sum(jnp.where(unsort[:, None] == slots_of[None, :], slots_of[:, None], 0), axis=0)
    o_sorted = jnp.take(my_order, perm)
    rs_sorted = jnp.take(my_order - position, perm)
    req_sorted = jnp.take(request, perm)
    q_sorted = jnp.take(query_rows, perm, axis=0)
    tables = attention_tables(o_sorted, rs_sorted, req_sorted)
    outs = []
    for head in range(local_heads):
        q_head = q_sorted[:, head].transpose(1, 0, 2)
        part = slice(head * 2 * HEAD_SIZE, (head + 1) * 2 * HEAD_SIZE)
        state = cache_attention(tables, q_head, req_sorted, cache[:, :, part])
        result = fresh_attention(tables, q_head, o_sorted, rs_sorted, state, kv_sorted[:, part])
        outs.append(result)
    outs = [jnp.take(result, unsort, axis=1).transpose(1, 0, 2) for result in outs]
    attn = jnp.stack(outs, axis=1).reshape(rows, local_heads * head_group * HEAD_SIZE)
    partial_value = jnp.dot(attn, w_out, preferred_element_type=jnp.float32)
    partial_value, arranged = lax.optimization_barrier((partial_value, arranged))
    decode_cache = lax.all_to_all(arranged, "seq", split_axis=1, concat_axis=2, tiled=True)
    attn_out = scatter_heads(partial_value)
    return (attn_out, decode_cache)


def solution(mesh):
    placed = (
        P("seq", "heads"),
        P(),
        P(),
        P(),
        P(),
        P(None, "heads"),
        P(None, "heads"),
        P(None, "heads"),
        P("heads", None),
        P(None, None, "seq", None, "heads"),
    )
    return jax.shard_map(
        on_device,
        mesh=mesh,
        in_specs=placed,
        out_specs=(P("seq", "heads"), P(None, "seq", None, None, "heads")),
        check_vma=False,
    )
```

```python
import jax
import jax.numpy as jnp
from jax import lax
from jax.sharding import PartitionSpec as P
import functools
from jax.experimental import pallas as pl
from jax.experimental.pallas import tpu as pltpu

QUERY_HEADS = 40
KEY_VALUE_HEADS = 8
HEAD_SIZE = 128
BLOCK_POSITIONS = 512
CB = 2


theta = 1000000.0
epsilon = 1e-06


def apply_rotary(value_rows, place):
    half = value_rows.shape[-1] // 2
    freq = theta ** (-2.0 * jnp.arange(half, dtype=jnp.float32) / value_rows.shape[-1])
    angle = place[:, None, None] * freq
    cosine = jnp.cos(angle)
    sine_part = jnp.sin(angle)
    first = value_rows[..., :half]
    second = value_rows[..., half:]
    return jnp.concatenate(
        [first * cosine - second * sine_part, second * cosine + first * sine_part], axis=-1
    )


def request_place(order, lengths):
    ends = jnp.cumsum(lengths)
    starts = ends - lengths
    request = jnp.sum((order[:, None] >= ends[None, :]).astype(jnp.int32), axis=1)
    labels = jnp.arange(lengths.shape[0], dtype=jnp.int32)
    begin = jnp.sum(jnp.where(request[:, None] == labels[None, :], starts[None, :], 0), axis=1)
    return (request, order - begin)


from jax.experimental import pallas as pl
from jax.experimental.pallas import tpu as pltpu

TILE = 16
CHUNK = 256


def _online(q, keys, values, mask, carry, scale):
    top, total, accum = carry
    width = keys.shape[0]
    scores = lax.dot_general(q, keys, (((1,), (1,)), ((), ())), preferred_element_type=jnp.float32) * scale
    scores = scores.reshape(-1, mask.shape[0], width)
    scores = jnp.where(mask[None], scores, -1e30).reshape(q.shape[0], width)
    new_top = jnp.maximum(top, jnp.max(scores, axis=1, keepdims=True))
    expo = jnp.exp(scores - new_top)
    fade = jnp.exp(top - new_top)
    total = total * fade + jnp.sum(expo, axis=1, keepdims=True)
    accum = accum * fade + jnp.dot(expo.astype(jnp.bfloat16), values, preferred_element_type=jnp.float32)
    return (new_top, total, accum)


def _cache_body(tables, q_ref, req_ref, cache_ref, top_ref, total_ref, accum_ref, *, scale):
    t = pl.program_id(0)
    group, rows, size = q_ref.shape
    q = q_ref[...].reshape(group * rows, size)
    req_row = req_ref[...]

    def cached(r, carry):
        mask = req_row == r
        for j in range(2):
            block = cache_ref[2 * r + j]
            carry = _online(q, block[:, :size], block[:, size:], mask, carry, scale)
        return carry

    carry = (
        jnp.full((group * rows, 1), -1e30, jnp.float32),
        jnp.zeros((group * rows, 1), jnp.float32),
        jnp.zeros((group * rows, size), jnp.float32),
    )
    top, total, accum = lax.fori_loop(tables[0, t], tables[1, t] + 1, cached, carry)
    top_ref[...] = top
    total_ref[...] = total
    accum_ref[...] = accum


def _fresh_body(tables, q_ref, o_ref, rs_ref, top_ref, total_ref, accum_ref, kv_ref, out_ref, *, scale):
    t = pl.program_id(0)
    group, rows, size = q_ref.shape
    q = q_ref[...].reshape(group * rows, size)
    o_row = o_ref[...]
    rs_row = rs_ref[...]

    def fresh(c, carry):
        start = pl.multiple_of(c * CHUNK, CHUNK)
        block = kv_ref[pl.ds(start, CHUNK), :]
        index = start + lax.broadcasted_iota(jnp.int32, (1, CHUNK), 1)
        mask = (index >= rs_row) & (index <= o_row)
        return _online(q, block[:, :size], block[:, size:], mask, carry, scale)

    carry = (top_ref[...], total_ref[...], accum_ref[...])
    top, total, accum = lax.fori_loop(tables[2, t], tables[3, t] + 1, fresh, carry)
    out_ref[...] = (accum / total).reshape(group, rows, size).astype(out_ref.dtype)


def attention_tables(o_sorted, rs_sorted, req_sorted):
    count = o_sorted.shape[0]
    firsts = jnp.arange(count // TILE) * TILE
    lasts = firsts + TILE - 1
    return jnp.stack([
        req_sorted[firsts], req_sorted[lasts], rs_sorted[firsts] // CHUNK, o_sorted[lasts] // CHUNK
    ]).astype(jnp.int32)


def cache_attention(tables, q_sorted, req_sorted, cache):
    group, count, size = q_sorted.shape
    tiles = count // TILE
    body = functools.partial(_cache_body, scale=size ** (-0.5))
    state = pl.BlockSpec((group * TILE, 1), lambda t, tb: (t, 0))
    spec = pltpu.PrefetchScalarGridSpec(
        num_scalar_prefetch=1,
        grid=(tiles,),
        in_specs=[
            pl.BlockSpec((group, TILE, size), lambda t, tb: (0, t, 0)),
            pl.BlockSpec((TILE, 1), lambda t, tb: (t, 0)),
            pl.BlockSpec(cache.shape, lambda t, tb: (0, 0, 0)),
        ],
        out_specs=[state, state, pl.BlockSpec((group * TILE, size), lambda t, tb: (t, 0))],
    )
    return pl.pallas_call(
        body,
        grid_spec=spec,
        out_shape=[
            jax.ShapeDtypeStruct((group * count, 1), jnp.float32),
            jax.ShapeDtypeStruct((group * count, 1), jnp.float32),
            jax.ShapeDtypeStruct((group * count, size), jnp.float32),
        ],
        compiler_params=pltpu.CompilerParams(dimension_semantics=("arbitrary",)),
    )(tables, q_sorted, req_sorted.reshape(count, 1), cache)


def fresh_attention(tables, q_sorted, o_sorted, rs_sorted, state, kv_sorted):
    group, count, size = q_sorted.shape
    tiles = count // TILE
    body = functools.partial(_fresh_body, scale=size ** (-0.5))
    column = pl.BlockSpec((TILE, 1), lambda t, tb: (t, 0))
    lane = pl.BlockSpec((group * TILE, 1), lambda t, tb: (t, 0))
    spec = pltpu.PrefetchScalarGridSpec(
        num_scalar_prefetch=1,
        grid=(tiles,),
        in_specs=[
            pl.BlockSpec((group, TILE, size), lambda t, tb: (0, t, 0)),
            column,
            column,
            lane,
            lane,
            pl.BlockSpec((group * TILE, size), lambda t, tb: (t, 0)),
            pl.BlockSpec(kv_sorted.shape, lambda t, tb: (0, 0)),
        ],
        out_specs=pl.BlockSpec((group, TILE, size), lambda t, tb: (0, t, 0)),
    )
    return pl.pallas_call(
        body,
        grid_spec=spec,
        out_shape=jax.ShapeDtypeStruct(q_sorted.shape, jnp.bfloat16),
        compiler_params=pltpu.CompilerParams(dimension_semantics=("arbitrary",)),
    )(tables, q_sorted, o_sorted.reshape(count, 1), rs_sorted.reshape(count, 1), *state, kv_sorted)


def rotate_columns(value, shift):
    doubled = jnp.concatenate([value, value], axis=1)
    return lax.dynamic_slice_in_dim(doubled, shift, value.shape[1], axis=1)


def gather_heads(piece):
    parts = lax.psum(1, "heads")
    me = lax.axis_index("heads")
    got = {0: piece}
    for shift in range(1, parts):
        pairs = [(i, (i + shift) % parts) for i in range(parts)]
        got[shift] = lax.ppermute(piece, "heads", pairs)
    ahead = jnp.concatenate([got[(parts - j) % parts] for j in range(parts)], axis=1)
    width = piece.shape[1]
    return rotate_columns(ahead, (parts - me) % parts * width)


def scatter_heads(partial_value):
    parts = lax.psum(1, "heads")
    me = lax.axis_index("heads")
    width = partial_value.shape[1] // parts
    ahead = rotate_columns(partial_value.astype(jnp.bfloat16), me * width)
    total = ahead[:, :width].astype(jnp.float32)
    for shift in range(1, parts):
        pairs = [(i, (i + shift) % parts) for i in range(parts)]
        piece = ahead[:, shift * width:(shift + 1) * width]
        total = total + lax.ppermute(piece, "heads", pairs).astype(jnp.float32)
    return total.astype(jnp.bfloat16)


def on_device(
    tokens,
    order,
    lengths,
    block_table,
    destination,
    w_query,
    key_weight,
    value_weight,
    w_out,
    key_value_cache,
):
    local_heads = key_weight.shape[1] // HEAD_SIZE
    slots = destination.shape[0]
    slot_labels = jnp.arange(slots, dtype=jnp.int32)
    inverse = jnp.sum(
        jnp.where(destination[None, :] == slot_labels[:, None], slot_labels[None, :], 0), axis=1
    )
    arranged = jnp.take(key_value_cache, inverse, axis=1)
    layer_zero = key_value_cache[0]
    used = jnp.take(layer_zero, block_table.reshape(-1), axis=0)
    pool, span = used.shape[0], used.shape[1]
    used = used.reshape(pool, span, 2, local_heads, HEAD_SIZE).transpose(0, 1, 3, 2, 4)
    used = used.reshape(pool, span, local_heads * 2 * HEAD_SIZE)
    cache = lax.all_gather(used, "seq", axis=1, tiled=True)
    by_order = jnp.argsort(order)
    full, arranged, cache, by_order = lax.optimization_barrier((gather_heads(tokens), arranged, cache, by_order))
    rows = full.shape[0]
    wide = full.astype(jnp.float32)
    normed = (wide * lax.rsqrt(jnp.mean(wide * wide, axis=1, keepdims=True) + epsilon)).astype(
        jnp.bfloat16
    )
    local_heads = key_weight.shape[1] // HEAD_SIZE
    head_group = QUERY_HEADS // KEY_VALUE_HEADS
    query_rows = jnp.dot(normed, w_query, preferred_element_type=jnp.float32)
    key_rows = jnp.dot(normed, key_weight, preferred_element_type=jnp.float32)
    value_rows = jnp.dot(normed, value_weight, preferred_element_type=jnp.float32)
    device = lax.axis_index("seq")
    my_order = lax.dynamic_slice_in_dim(order, device * rows, rows)
    request, position = request_place(my_order, lengths)
    rotary_angles = (position + CB * BLOCK_POSITIONS).astype(jnp.float32)
    query_rows = apply_rotary(
        query_rows.reshape(rows, local_heads * head_group, HEAD_SIZE), rotary_angles
    ).astype(jnp.bfloat16)
    query_rows = query_rows.reshape(rows, local_heads, head_group, HEAD_SIZE)
    key_rows = (
        apply_rotary(key_rows.reshape(rows, local_heads, HEAD_SIZE), rotary_angles)
        .astype(jnp.bfloat16)
        .reshape(rows, local_heads * HEAD_SIZE)
    )
    fresh_rows = jnp.concatenate(
        [
            key_rows.reshape(rows, local_heads, HEAD_SIZE),
            value_rows.astype(jnp.bfloat16).reshape(rows, local_heads, HEAD_SIZE),
        ],
        axis=2,
    ).reshape(rows, local_heads * 2 * HEAD_SIZE)
    gathered = lax.all_gather(fresh_rows, "seq", axis=0, tiled=True)
    gathered, arranged = lax.optimization_barrier((gathered, arranged))
    decode_cache = lax.all_to_all(arranged, "seq", split_axis=1, concat_axis=2, tiled=True)
    kv_sorted = jnp.take(gathered, by_order, axis=0)
    earlier = (my_order[None, :] < my_order[:, None]).astype(jnp.int32)
    unsort = jnp.sum(earlier, axis=1)
    slots_of = jnp.arange(rows, dtype=jnp.int32)
    perm = jnp.sum(jnp.where(unsort[:, None] == slots_of[None, :], slots_of[:, None], 0), axis=0)
    o_sorted = jnp.take(my_order, perm)
    rs_sorted = jnp.take(my_order - position, perm)
    req_sorted = jnp.take(request, perm)
    q_sorted = jnp.take(query_rows, perm, axis=0)
    tables = attention_tables(o_sorted, rs_sorted, req_sorted)
    outs = []
    for head in range(local_heads):
        q_head = q_sorted[:, head].transpose(1, 0, 2)
        part = slice(head * 2 * HEAD_SIZE, (head + 1) * 2 * HEAD_SIZE)
        state = cache_attention(tables, q_head, req_sorted, cache[:, :, part])
        result = fresh_attention(tables, q_head, o_sorted, rs_sorted, state, kv_sorted[:, part])
        outs.append(result)
    outs = [jnp.take(result, unsort, axis=1).transpose(1, 0, 2) for result in outs]
    attn = jnp.stack(outs, axis=1).reshape(rows, local_heads * head_group * HEAD_SIZE)
    partial_value = jnp.dot(attn, w_out, preferred_element_type=jnp.float32)
    attn_out = scatter_heads(partial_value)
    return (attn_out, decode_cache)


def solution(mesh):
    placed = (
        P("seq", "heads"),
        P(),
        P(),
        P(),
        P(),
        P(None, "heads"),
        P(None, "heads"),
        P(None, "heads"),
        P("heads", None),
        P(None, None, "seq", None, "heads"),
    )
    return jax.shard_map(
        on_device,
        mesh=mesh,
        in_specs=placed,
        out_specs=(P("seq", "heads"), P(None, "seq", None, None, "heads")),
        check_vma=False,
    )
```

```python
import jax
import jax.numpy as jnp
from jax import lax
from jax.sharding import PartitionSpec as P
import functools
from jax.experimental import pallas as pl
from jax.experimental.pallas import tpu as pltpu

QUERY_HEADS = 40
KEY_VALUE_HEADS = 8
HEAD_SIZE = 128
BLOCK_POSITIONS = 512
CB = 2


theta = 1000000.0
epsilon = 1e-06


def apply_rotary(value_rows, place):
    half = value_rows.shape[-1] // 2
    freq = theta ** (-2.0 * jnp.arange(half, dtype=jnp.float32) / value_rows.shape[-1])
    angle = place[:, None, None] * freq
    cosine = jnp.cos(angle)
    sine_part = jnp.sin(angle)
    first = value_rows[..., :half]
    second = value_rows[..., half:]
    return jnp.concatenate(
        [first * cosine - second * sine_part, second * cosine + first * sine_part], axis=-1
    )


def request_place(order, lengths):
    ends = jnp.cumsum(lengths)
    starts = ends - lengths
    request = jnp.sum((order[:, None] >= ends[None, :]).astype(jnp.int32), axis=1)
    labels = jnp.arange(lengths.shape[0], dtype=jnp.int32)
    begin = jnp.sum(jnp.where(request[:, None] == labels[None, :], starts[None, :], 0), axis=1)
    return (request, order - begin)


from jax.experimental import pallas as pl
from jax.experimental.pallas import tpu as pltpu

TILE = 32
CHUNK = 512


def _online(q, keys, values, mask, carry, scale):
    top, total, accum = carry
    width = keys.shape[0]
    scores = lax.dot_general(q, keys, (((1,), (1,)), ((), ())), preferred_element_type=jnp.float32) * scale
    scores = scores.reshape(-1, mask.shape[0], width)
    scores = jnp.where(mask[None], scores, -1e30).reshape(q.shape[0], width)
    new_top = jnp.maximum(top, jnp.max(scores, axis=1, keepdims=True))
    expo = jnp.exp(scores - new_top)
    fade = jnp.exp(top - new_top)
    total = total * fade + jnp.sum(expo, axis=1, keepdims=True)
    accum = accum * fade + jnp.dot(expo.astype(jnp.bfloat16), values, preferred_element_type=jnp.float32)
    return (new_top, total, accum)


def _cache_body(tables, q_ref, req_ref, cache_ref, top_ref, total_ref, accum_ref, *, scale):
    t = pl.program_id(0)
    group, rows, size = q_ref.shape
    q = q_ref[...].reshape(group * rows, size)
    req_row = req_ref[...]

    def cached(r, carry):
        mask = req_row == r
        block = jnp.concatenate([cache_ref[2 * r], cache_ref[2 * r + 1]], axis=0)
        return _online(q, block[:, :size], block[:, size:], mask, carry, scale)

    carry = (
        jnp.full((group * rows, 1), -1e30, jnp.float32),
        jnp.zeros((group * rows, 1), jnp.float32),
        jnp.zeros((group * rows, size), jnp.float32),
    )
    top, total, accum = lax.fori_loop(tables[0, t], tables[1, t] + 1, cached, carry)
    top_ref[...] = top
    total_ref[...] = total
    accum_ref[...] = accum


def _fresh_body(tables, q_ref, o_ref, rs_ref, top_ref, total_ref, accum_ref, kv_ref, out_ref, *, scale):
    t = pl.program_id(0)
    group, rows, size = q_ref.shape
    q = q_ref[...].reshape(group * rows, size)
    o_row = o_ref[...]
    rs_row = rs_ref[...]

    def fresh(c, carry):
        start = pl.multiple_of(c * CHUNK, CHUNK)
        block = kv_ref[pl.ds(start, CHUNK), :]
        index = start + lax.broadcasted_iota(jnp.int32, (1, CHUNK), 1)
        mask = (index >= rs_row) & (index <= o_row)
        return _online(q, block[:, :size], block[:, size:], mask, carry, scale)

    carry = (top_ref[...], total_ref[...], accum_ref[...])
    top, total, accum = lax.fori_loop(tables[2, t], tables[3, t] + 1, fresh, carry)
    out_ref[...] = (accum / total).reshape(group, rows, size).astype(out_ref.dtype)


def attention_tables(o_sorted, rs_sorted, req_sorted):
    count = o_sorted.shape[0]
    firsts = jnp.arange(count // TILE) * TILE
    lasts = firsts + TILE - 1
    return jnp.stack([
        req_sorted[firsts], req_sorted[lasts], rs_sorted[firsts] // CHUNK, o_sorted[lasts] // CHUNK
    ]).astype(jnp.int32)


def cache_attention(tables, q_sorted, req_sorted, cache):
    group, count, size = q_sorted.shape
    tiles = count // TILE
    body = functools.partial(_cache_body, scale=size ** (-0.5))
    state = pl.BlockSpec((group * TILE, 1), lambda t, tb: (t, 0))
    spec = pltpu.PrefetchScalarGridSpec(
        num_scalar_prefetch=1,
        grid=(tiles,),
        in_specs=[
            pl.BlockSpec((group, TILE, size), lambda t, tb: (0, t, 0)),
            pl.BlockSpec((TILE, 1), lambda t, tb: (t, 0)),
            pl.BlockSpec(cache.shape, lambda t, tb: (0, 0, 0)),
        ],
        out_specs=[state, state, pl.BlockSpec((group * TILE, size), lambda t, tb: (t, 0))],
    )
    return pl.pallas_call(
        body,
        grid_spec=spec,
        out_shape=[
            jax.ShapeDtypeStruct((group * count, 1), jnp.float32),
            jax.ShapeDtypeStruct((group * count, 1), jnp.float32),
            jax.ShapeDtypeStruct((group * count, size), jnp.float32),
        ],
        compiler_params=pltpu.CompilerParams(dimension_semantics=("arbitrary",)),
    )(tables, q_sorted, req_sorted.reshape(count, 1), cache)


def fresh_attention(tables, q_sorted, o_sorted, rs_sorted, state, kv_sorted):
    group, count, size = q_sorted.shape
    tiles = count // TILE
    body = functools.partial(_fresh_body, scale=size ** (-0.5))
    column = pl.BlockSpec((TILE, 1), lambda t, tb: (t, 0))
    lane = pl.BlockSpec((group * TILE, 1), lambda t, tb: (t, 0))
    spec = pltpu.PrefetchScalarGridSpec(
        num_scalar_prefetch=1,
        grid=(tiles,),
        in_specs=[
            pl.BlockSpec((group, TILE, size), lambda t, tb: (0, t, 0)),
            column,
            column,
            lane,
            lane,
            pl.BlockSpec((group * TILE, size), lambda t, tb: (t, 0)),
            pl.BlockSpec(kv_sorted.shape, lambda t, tb: (0, 0)),
        ],
        out_specs=pl.BlockSpec((group, TILE, size), lambda t, tb: (0, t, 0)),
    )
    return pl.pallas_call(
        body,
        grid_spec=spec,
        out_shape=jax.ShapeDtypeStruct(q_sorted.shape, jnp.bfloat16),
        compiler_params=pltpu.CompilerParams(dimension_semantics=("arbitrary",)),
    )(tables, q_sorted, o_sorted.reshape(count, 1), rs_sorted.reshape(count, 1), *state, kv_sorted)


def rotate_columns(value, shift):
    doubled = jnp.concatenate([value, value], axis=1)
    return lax.dynamic_slice_in_dim(doubled, shift, value.shape[1], axis=1)


def gather_heads(piece):
    parts = lax.psum(1, "heads")
    me = lax.axis_index("heads")
    got = {0: piece}
    for shift in range(1, parts):
        pairs = [(i, (i + shift) % parts) for i in range(parts)]
        got[shift] = lax.ppermute(piece, "heads", pairs)
    ahead = jnp.concatenate([got[(parts - j) % parts] for j in range(parts)], axis=1)
    width = piece.shape[1]
    return rotate_columns(ahead, (parts - me) % parts * width)


def scatter_heads(partial_value):
    parts = lax.psum(1, "heads")
    me = lax.axis_index("heads")
    width = partial_value.shape[1] // parts
    ahead = rotate_columns(partial_value.astype(jnp.bfloat16), me * width)
    total = ahead[:, :width].astype(jnp.float32)
    for shift in range(1, parts):
        pairs = [(i, (i + shift) % parts) for i in range(parts)]
        piece = ahead[:, shift * width:(shift + 1) * width]
        total = total + lax.ppermute(piece, "heads", pairs).astype(jnp.float32)
    return total.astype(jnp.bfloat16)


def on_device(
    tokens,
    order,
    lengths,
    block_table,
    destination,
    w_query,
    key_weight,
    value_weight,
    w_out,
    key_value_cache,
):
    local_heads = key_weight.shape[1] // HEAD_SIZE
    slots = destination.shape[0]
    slot_labels = jnp.arange(slots, dtype=jnp.int32)
    inverse = jnp.sum(
        jnp.where(destination[None, :] == slot_labels[:, None], slot_labels[None, :], 0), axis=1
    )
    arranged = jnp.take(key_value_cache, inverse, axis=1)
    layer_zero = key_value_cache[0]
    used = jnp.take(layer_zero, block_table.reshape(-1), axis=0)
    pool, span = used.shape[0], used.shape[1]
    used = used.reshape(pool, span, 2, local_heads, HEAD_SIZE).transpose(0, 1, 3, 2, 4)
    used = used.reshape(pool, span, local_heads * 2 * HEAD_SIZE)
    cache = lax.all_gather(used, "seq", axis=1, tiled=True)
    by_order = jnp.argsort(order)
    full, arranged, cache, by_order = lax.optimization_barrier((gather_heads(tokens), arranged, cache, by_order))
    rows = full.shape[0]
    wide = full.astype(jnp.float32)
    normed = (wide * lax.rsqrt(jnp.mean(wide * wide, axis=1, keepdims=True) + epsilon)).astype(
        jnp.bfloat16
    )
    local_heads = key_weight.shape[1] // HEAD_SIZE
    head_group = QUERY_HEADS // KEY_VALUE_HEADS
    query_rows = jnp.dot(normed, w_query, preferred_element_type=jnp.float32)
    key_rows = jnp.dot(normed, key_weight, preferred_element_type=jnp.float32)
    value_rows = jnp.dot(normed, value_weight, preferred_element_type=jnp.float32)
    device = lax.axis_index("seq")
    my_order = lax.dynamic_slice_in_dim(order, device * rows, rows)
    request, position = request_place(my_order, lengths)
    rotary_angles = (position + CB * BLOCK_POSITIONS).astype(jnp.float32)
    query_rows = apply_rotary(
        query_rows.reshape(rows, local_heads * head_group, HEAD_SIZE), rotary_angles
    ).astype(jnp.bfloat16)
    query_rows = query_rows.reshape(rows, local_heads, head_group, HEAD_SIZE)
    key_rows = (
        apply_rotary(key_rows.reshape(rows, local_heads, HEAD_SIZE), rotary_angles)
        .astype(jnp.bfloat16)
        .reshape(rows, local_heads * HEAD_SIZE)
    )
    fresh_rows = jnp.concatenate(
        [
            key_rows.reshape(rows, local_heads, HEAD_SIZE),
            value_rows.astype(jnp.bfloat16).reshape(rows, local_heads, HEAD_SIZE),
        ],
        axis=2,
    ).reshape(rows, local_heads * 2 * HEAD_SIZE)
    gathered = lax.all_gather(fresh_rows, "seq", axis=0, tiled=True)
    gathered, arranged = lax.optimization_barrier((gathered, arranged))
    decode_cache = lax.all_to_all(arranged, "seq", split_axis=1, concat_axis=2, tiled=True)
    kv_sorted = jnp.take(gathered, by_order, axis=0)
    earlier = (my_order[None, :] < my_order[:, None]).astype(jnp.int32)
    unsort = jnp.sum(earlier, axis=1)
    slots_of = jnp.arange(rows, dtype=jnp.int32)
    perm = jnp.sum(jnp.where(unsort[:, None] == slots_of[None, :], slots_of[:, None], 0), axis=0)
    o_sorted = jnp.take(my_order, perm)
    rs_sorted = jnp.take(my_order - position, perm)
    req_sorted = jnp.take(request, perm)
    q_sorted = jnp.take(query_rows, perm, axis=0)
    tables = attention_tables(o_sorted, rs_sorted, req_sorted)
    outs = []
    for head in range(local_heads):
        q_head = q_sorted[:, head].transpose(1, 0, 2)
        part = slice(head * 2 * HEAD_SIZE, (head + 1) * 2 * HEAD_SIZE)
        state = cache_attention(tables, q_head, req_sorted, cache[:, :, part])
        result = fresh_attention(tables, q_head, o_sorted, rs_sorted, state, kv_sorted[:, part])
        outs.append(result)
    outs = [jnp.take(result, unsort, axis=1).transpose(1, 0, 2) for result in outs]
    attn = jnp.stack(outs, axis=1).reshape(rows, local_heads * head_group * HEAD_SIZE)
    partial_value = jnp.dot(attn, w_out, preferred_element_type=jnp.float32)
    attn_out = scatter_heads(partial_value)
    return (attn_out, decode_cache)


def solution(mesh):
    placed = (
        P("seq", "heads"),
        P(),
        P(),
        P(),
        P(),
        P(None, "heads"),
        P(None, "heads"),
        P(None, "heads"),
        P("heads", None),
        P(None, None, "seq", None, "heads"),
    )
    return jax.shard_map(
        on_device,
        mesh=mesh,
        in_specs=placed,
        out_specs=(P("seq", "heads"), P(None, "seq", None, None, "heads")),
        check_vma=False,
    )
```

```python
import jax
import jax.numpy as jnp
from jax import lax
from jax.sharding import PartitionSpec as P
import functools
from jax.experimental import pallas as pl
from jax.experimental.pallas import tpu as pltpu

QUERY_HEADS = 40
KEY_VALUE_HEADS = 8
HEAD_SIZE = 128
BLOCK_POSITIONS = 512
CB = 2


theta = 1000000.0
epsilon = 1e-06


def apply_rotary(value_rows, place):
    half = value_rows.shape[-1] // 2
    freq = theta ** (-2.0 * jnp.arange(half, dtype=jnp.float32) / value_rows.shape[-1])
    angle = place[:, None, None] * freq
    cosine = jnp.cos(angle)
    sine_part = jnp.sin(angle)
    first = value_rows[..., :half]
    second = value_rows[..., half:]
    return jnp.concatenate(
        [first * cosine - second * sine_part, second * cosine + first * sine_part], axis=-1
    )


def request_place(order, lengths):
    ends = jnp.cumsum(lengths)
    starts = ends - lengths
    request = jnp.sum((order[:, None] >= ends[None, :]).astype(jnp.int32), axis=1)
    labels = jnp.arange(lengths.shape[0], dtype=jnp.int32)
    begin = jnp.sum(jnp.where(request[:, None] == labels[None, :], starts[None, :], 0), axis=1)
    return (request, order - begin)


from jax.experimental import pallas as pl
from jax.experimental.pallas import tpu as pltpu

TILE = 32
CHUNK = 512


def _online(q, keys, values, mask, carry, scale):
    top, total, accum = carry
    width = keys.shape[0]
    scores = lax.dot_general(q, keys, (((1,), (1,)), ((), ())), preferred_element_type=jnp.float32) * scale
    scores = scores.reshape(-1, mask.shape[0], width)
    scores = jnp.where(mask[None], scores, -1e30).reshape(q.shape[0], width)
    new_top = jnp.maximum(top, jnp.max(scores, axis=1, keepdims=True))
    expo = jnp.exp(scores - new_top)
    fade = jnp.exp(top - new_top)
    total = total * fade + jnp.sum(expo, axis=1, keepdims=True)
    accum = accum * fade + jnp.dot(expo.astype(jnp.bfloat16), values, preferred_element_type=jnp.float32)
    return (new_top, total, accum)


def _cache_body(tables, q_ref, req_ref, cache_ref, top_ref, total_ref, accum_ref, *, scale):
    t = pl.program_id(0)
    group, rows, size = q_ref.shape
    q = q_ref[...].reshape(group * rows, size)
    req_row = req_ref[...]

    def cached(r, carry):
        mask = req_row == r
        block = jnp.concatenate([cache_ref[2 * r], cache_ref[2 * r + 1]], axis=0)
        return _online(q, block[:, :size], block[:, size:], mask, carry, scale)

    carry = (
        jnp.full((group * rows, 1), -1e30, jnp.float32),
        jnp.zeros((group * rows, 1), jnp.float32),
        jnp.zeros((group * rows, size), jnp.float32),
    )
    top, total, accum = lax.fori_loop(tables[0, t], tables[1, t] + 1, cached, carry)
    top_ref[...] = top
    total_ref[...] = total
    accum_ref[...] = accum


def _fresh_body(tables, q_ref, o_ref, rs_ref, top_ref, total_ref, accum_ref, kv_ref, out_ref, *, scale):
    t = pl.program_id(0)
    group, rows, size = q_ref.shape
    q = q_ref[...].reshape(group * rows, size)
    o_row = o_ref[...]
    rs_row = rs_ref[...]

    def fresh(c, carry):
        start = pl.multiple_of(c * CHUNK, CHUNK)
        block = kv_ref[pl.ds(start, CHUNK), :]
        index = start + lax.broadcasted_iota(jnp.int32, (1, CHUNK), 1)
        mask = (index >= rs_row) & (index <= o_row)
        return _online(q, block[:, :size], block[:, size:], mask, carry, scale)

    carry = (top_ref[...], total_ref[...], accum_ref[...])
    top, total, accum = lax.fori_loop(tables[2, t], tables[3, t] + 1, fresh, carry)
    out_ref[...] = (accum / total).reshape(group, rows, size).astype(out_ref.dtype)


def attention_tables(o_sorted, rs_sorted, req_sorted):
    count = o_sorted.shape[0]
    firsts = jnp.arange(count // TILE) * TILE
    lasts = firsts + TILE - 1
    return jnp.stack([
        req_sorted[firsts], req_sorted[lasts], rs_sorted[firsts] // CHUNK, o_sorted[lasts] // CHUNK
    ]).astype(jnp.int32)


def cache_attention(tables, q_sorted, req_sorted, cache):
    group, count, size = q_sorted.shape
    tiles = count // TILE
    body = functools.partial(_cache_body, scale=size ** (-0.5))
    state = pl.BlockSpec((group * TILE, 1), lambda t, tb: (t, 0))
    spec = pltpu.PrefetchScalarGridSpec(
        num_scalar_prefetch=1,
        grid=(tiles,),
        in_specs=[
            pl.BlockSpec((group, TILE, size), lambda t, tb: (0, t, 0)),
            pl.BlockSpec((TILE, 1), lambda t, tb: (t, 0)),
            pl.BlockSpec(cache.shape, lambda t, tb: (0, 0, 0)),
        ],
        out_specs=[state, state, pl.BlockSpec((group * TILE, size), lambda t, tb: (t, 0))],
    )
    return pl.pallas_call(
        body,
        grid_spec=spec,
        out_shape=[
            jax.ShapeDtypeStruct((group * count, 1), jnp.float32),
            jax.ShapeDtypeStruct((group * count, 1), jnp.float32),
            jax.ShapeDtypeStruct((group * count, size), jnp.float32),
        ],
        compiler_params=pltpu.CompilerParams(dimension_semantics=("arbitrary",)),
    )(tables, q_sorted, req_sorted.reshape(count, 1), cache)


def fresh_attention(tables, q_sorted, o_sorted, rs_sorted, state, kv_sorted):
    group, count, size = q_sorted.shape
    tiles = count // TILE
    body = functools.partial(_fresh_body, scale=size ** (-0.5))
    column = pl.BlockSpec((TILE, 1), lambda t, tb: (t, 0))
    lane = pl.BlockSpec((group * TILE, 1), lambda t, tb: (t, 0))
    spec = pltpu.PrefetchScalarGridSpec(
        num_scalar_prefetch=1,
        grid=(tiles,),
        in_specs=[
            pl.BlockSpec((group, TILE, size), lambda t, tb: (0, t, 0)),
            column,
            column,
            lane,
            lane,
            pl.BlockSpec((group * TILE, size), lambda t, tb: (t, 0)),
            pl.BlockSpec(kv_sorted.shape, lambda t, tb: (0, 0)),
        ],
        out_specs=pl.BlockSpec((group, TILE, size), lambda t, tb: (0, t, 0)),
    )
    return pl.pallas_call(
        body,
        grid_spec=spec,
        out_shape=jax.ShapeDtypeStruct(q_sorted.shape, jnp.bfloat16),
        compiler_params=pltpu.CompilerParams(dimension_semantics=("arbitrary",)),
    )(tables, q_sorted, o_sorted.reshape(count, 1), rs_sorted.reshape(count, 1), *state, kv_sorted)


def rotate_columns(value, shift):
    doubled = jnp.concatenate([value, value], axis=1)
    return lax.dynamic_slice_in_dim(doubled, shift, value.shape[1], axis=1)


def gather_heads(piece):
    parts = lax.psum(1, "heads")
    me = lax.axis_index("heads")
    width = piece.shape[1]
    full = jnp.zeros((piece.shape[0], parts * width), piece.dtype)
    for shift in range(parts):
        got = piece
        if shift > 0:
            pairs = [(i, (i + shift) % parts) for i in range(parts)]
            got = lax.ppermute(piece, "heads", pairs)
        source = lax.rem(me - shift + parts, parts)
        full = lax.dynamic_update_slice_in_dim(full, got, source * width, axis=1)
    return full


def scatter_heads(partial_value):
    parts = lax.psum(1, "heads")
    me = lax.axis_index("heads")
    width = partial_value.shape[1] // parts
    ahead = rotate_columns(partial_value.astype(jnp.bfloat16), me * width)
    total = ahead[:, :width].astype(jnp.float32)
    for shift in range(1, parts):
        pairs = [(i, (i + shift) % parts) for i in range(parts)]
        piece = ahead[:, shift * width:(shift + 1) * width]
        total = total + lax.ppermute(piece, "heads", pairs).astype(jnp.float32)
    return total.astype(jnp.bfloat16)


def on_device(
    tokens,
    order,
    lengths,
    block_table,
    destination,
    w_query,
    key_weight,
    value_weight,
    w_out,
    key_value_cache,
):
    local_heads = key_weight.shape[1] // HEAD_SIZE
    slots = destination.shape[0]
    slot_labels = jnp.arange(slots, dtype=jnp.int32)
    inverse = jnp.sum(
        jnp.where(destination[None, :] == slot_labels[:, None], slot_labels[None, :], 0), axis=1
    )
    arranged = jnp.take(key_value_cache, inverse, axis=1)
    layer_zero = key_value_cache[0]
    used = jnp.take(layer_zero, block_table.reshape(-1), axis=0)
    pool, span = used.shape[0], used.shape[1]
    used = used.reshape(pool, span, 2, local_heads, HEAD_SIZE).transpose(0, 1, 3, 2, 4)
    used = used.reshape(pool, span, local_heads * 2 * HEAD_SIZE)
    cache = lax.all_gather(used, "seq", axis=1, tiled=True)
    by_order = jnp.argsort(order)
    full, arranged, cache, by_order = lax.optimization_barrier((gather_heads(tokens), arranged, cache, by_order))
    rows = full.shape[0]
    wide = full.astype(jnp.float32)
    normed = (wide * lax.rsqrt(jnp.mean(wide * wide, axis=1, keepdims=True) + epsilon)).astype(
        jnp.bfloat16
    )
    local_heads = key_weight.shape[1] // HEAD_SIZE
    head_group = QUERY_HEADS // KEY_VALUE_HEADS
    query_rows = jnp.dot(normed, w_query, preferred_element_type=jnp.float32)
    key_rows = jnp.dot(normed, key_weight, preferred_element_type=jnp.float32)
    value_rows = jnp.dot(normed, value_weight, preferred_element_type=jnp.float32)
    device = lax.axis_index("seq")
    my_order = lax.dynamic_slice_in_dim(order, device * rows, rows)
    request, position = request_place(my_order, lengths)
    rotary_angles = (position + CB * BLOCK_POSITIONS).astype(jnp.float32)
    query_rows = apply_rotary(
        query_rows.reshape(rows, local_heads * head_group, HEAD_SIZE), rotary_angles
    ).astype(jnp.bfloat16)
    query_rows = query_rows.reshape(rows, local_heads, head_group, HEAD_SIZE)
    key_rows = (
        apply_rotary(key_rows.reshape(rows, local_heads, HEAD_SIZE), rotary_angles)
        .astype(jnp.bfloat16)
        .reshape(rows, local_heads * HEAD_SIZE)
    )
    fresh_rows = jnp.concatenate(
        [
            key_rows.reshape(rows, local_heads, HEAD_SIZE),
            value_rows.astype(jnp.bfloat16).reshape(rows, local_heads, HEAD_SIZE),
        ],
        axis=2,
    ).reshape(rows, local_heads * 2 * HEAD_SIZE)
    gathered = lax.all_gather(fresh_rows, "seq", axis=0, tiled=True)
    gathered, arranged = lax.optimization_barrier((gathered, arranged))
    decode_cache = lax.all_to_all(arranged, "seq", split_axis=1, concat_axis=2, tiled=True)
    kv_sorted = jnp.take(gathered, by_order, axis=0)
    earlier = (my_order[None, :] < my_order[:, None]).astype(jnp.int32)
    unsort = jnp.sum(earlier, axis=1)
    slots_of = jnp.arange(rows, dtype=jnp.int32)
    perm = jnp.sum(jnp.where(unsort[:, None] == slots_of[None, :], slots_of[:, None], 0), axis=0)
    o_sorted = jnp.take(my_order, perm)
    rs_sorted = jnp.take(my_order - position, perm)
    req_sorted = jnp.take(request, perm)
    q_sorted = jnp.take(query_rows, perm, axis=0)
    tables = attention_tables(o_sorted, rs_sorted, req_sorted)
    outs = []
    for head in range(local_heads):
        q_head = q_sorted[:, head].transpose(1, 0, 2)
        part = slice(head * 2 * HEAD_SIZE, (head + 1) * 2 * HEAD_SIZE)
        state = cache_attention(tables, q_head, req_sorted, cache[:, :, part])
        result = fresh_attention(tables, q_head, o_sorted, rs_sorted, state, kv_sorted[:, part])
        outs.append(result)
    outs = [jnp.take(result, unsort, axis=1).transpose(1, 0, 2) for result in outs]
    attn = jnp.stack(outs, axis=1).reshape(rows, local_heads * head_group * HEAD_SIZE)
    partial_value = jnp.dot(attn, w_out, preferred_element_type=jnp.float32)
    attn_out = scatter_heads(partial_value)
    return (attn_out, decode_cache)


def solution(mesh):
    placed = (
        P("seq", "heads"),
        P(),
        P(),
        P(),
        P(),
        P(None, "heads"),
        P(None, "heads"),
        P(None, "heads"),
        P("heads", None),
        P(None, None, "seq", None, "heads"),
    )
    return jax.shard_map(
        on_device,
        mesh=mesh,
        in_specs=placed,
        out_specs=(P("seq", "heads"), P(None, "seq", None, None, "heads")),
        check_vma=False,
    )
```

```python
import jax
import jax.numpy as jnp
from jax import lax
from jax.sharding import PartitionSpec as P
import functools
from jax.experimental import pallas as pl
from jax.experimental.pallas import tpu as pltpu

QUERY_HEADS = 40
KEY_VALUE_HEADS = 8
HEAD_SIZE = 128
BLOCK_POSITIONS = 512
CB = 2


theta = 1000000.0
epsilon = 1e-06


def apply_rotary(value_rows, place):
    half = value_rows.shape[-1] // 2
    freq = theta ** (-2.0 * jnp.arange(half, dtype=jnp.float32) / value_rows.shape[-1])
    angle = place[:, None, None] * freq
    cosine = jnp.cos(angle)
    sine_part = jnp.sin(angle)
    first = value_rows[..., :half]
    second = value_rows[..., half:]
    return jnp.concatenate(
        [first * cosine - second * sine_part, second * cosine + first * sine_part], axis=-1
    )


def request_place(order, lengths):
    ends = jnp.cumsum(lengths)
    starts = ends - lengths
    request = jnp.sum((order[:, None] >= ends[None, :]).astype(jnp.int32), axis=1)
    labels = jnp.arange(lengths.shape[0], dtype=jnp.int32)
    begin = jnp.sum(jnp.where(request[:, None] == labels[None, :], starts[None, :], 0), axis=1)
    return (request, order - begin)


from jax.experimental import pallas as pl
from jax.experimental.pallas import tpu as pltpu

TILE = 32
CHUNK = 512


def _online(q, keys, values, mask, carry, scale):
    top, total, accum = carry
    width = keys.shape[0]
    scores = lax.dot_general(q, keys, (((1,), (1,)), ((), ())), preferred_element_type=jnp.float32) * scale
    scores = scores.reshape(-1, mask.shape[0], width)
    scores = jnp.where(mask[None], scores, -1e30).reshape(q.shape[0], width)
    new_top = jnp.maximum(top, jnp.max(scores, axis=1, keepdims=True))
    expo = jnp.exp(scores - new_top)
    fade = jnp.exp(top - new_top)
    total = total * fade + jnp.sum(expo, axis=1, keepdims=True)
    accum = accum * fade + jnp.dot(expo.astype(jnp.bfloat16), values, preferred_element_type=jnp.float32)
    return (new_top, total, accum)


def _cache_body(tables, q_ref, req_ref, cache_ref, top_ref, total_ref, accum_ref, *, scale):
    t = pl.program_id(0)
    group, rows, size = q_ref.shape
    q = q_ref[...].reshape(group * rows, size)
    req_row = req_ref[...]

    def cached(r, carry):
        mask = req_row == r
        block = jnp.concatenate([cache_ref[2 * r], cache_ref[2 * r + 1]], axis=0)
        return _online(q, block[:, :size], block[:, size:], mask, carry, scale)

    carry = (
        jnp.full((group * rows, 1), -1e30, jnp.float32),
        jnp.zeros((group * rows, 1), jnp.float32),
        jnp.zeros((group * rows, size), jnp.float32),
    )
    top, total, accum = lax.fori_loop(tables[0, t], tables[1, t] + 1, cached, carry)
    top_ref[...] = top
    total_ref[...] = total
    accum_ref[...] = accum


def _fresh_body(tables, q_ref, o_ref, rs_ref, top_ref, total_ref, accum_ref, kv_ref, out_ref, *, scale):
    t = pl.program_id(0)
    group, rows, size = q_ref.shape
    q = q_ref[...].reshape(group * rows, size)
    o_row = o_ref[...]
    rs_row = rs_ref[...]

    def fresh(c, carry):
        start = pl.multiple_of(c * CHUNK, CHUNK)
        block = kv_ref[pl.ds(start, CHUNK), :]
        index = start + lax.broadcasted_iota(jnp.int32, (1, CHUNK), 1)
        mask = (index >= rs_row) & (index <= o_row)
        return _online(q, block[:, :size], block[:, size:], mask, carry, scale)

    carry = (top_ref[...], total_ref[...], accum_ref[...])
    top, total, accum = lax.fori_loop(tables[2, t], tables[3, t] + 1, fresh, carry)
    out_ref[...] = (accum / total).reshape(group, rows, size).astype(out_ref.dtype)


def attention_tables(o_sorted, rs_sorted, req_sorted):
    count = o_sorted.shape[0]
    firsts = jnp.arange(count // TILE) * TILE
    lasts = firsts + TILE - 1
    return jnp.stack([
        req_sorted[firsts], req_sorted[lasts], rs_sorted[firsts] // CHUNK, o_sorted[lasts] // CHUNK
    ]).astype(jnp.int32)


def cache_attention(tables, q_sorted, req_sorted, cache):
    group, count, size = q_sorted.shape
    tiles = count // TILE
    body = functools.partial(_cache_body, scale=size ** (-0.5))
    state = pl.BlockSpec((group * TILE, 1), lambda t, tb: (t, 0))
    spec = pltpu.PrefetchScalarGridSpec(
        num_scalar_prefetch=1,
        grid=(tiles,),
        in_specs=[
            pl.BlockSpec((group, TILE, size), lambda t, tb: (0, t, 0)),
            pl.BlockSpec((TILE, 1), lambda t, tb: (t, 0)),
            pl.BlockSpec(cache.shape, lambda t, tb: (0, 0, 0)),
        ],
        out_specs=[state, state, pl.BlockSpec((group * TILE, size), lambda t, tb: (t, 0))],
    )
    return pl.pallas_call(
        body,
        grid_spec=spec,
        out_shape=[
            jax.ShapeDtypeStruct((group * count, 1), jnp.float32),
            jax.ShapeDtypeStruct((group * count, 1), jnp.float32),
            jax.ShapeDtypeStruct((group * count, size), jnp.float32),
        ],
        compiler_params=pltpu.CompilerParams(dimension_semantics=("arbitrary",)),
    )(tables, q_sorted, req_sorted.reshape(count, 1), cache)


def fresh_attention(tables, q_sorted, o_sorted, rs_sorted, state, kv_sorted):
    group, count, size = q_sorted.shape
    tiles = count // TILE
    body = functools.partial(_fresh_body, scale=size ** (-0.5))
    column = pl.BlockSpec((TILE, 1), lambda t, tb: (t, 0))
    lane = pl.BlockSpec((group * TILE, 1), lambda t, tb: (t, 0))
    spec = pltpu.PrefetchScalarGridSpec(
        num_scalar_prefetch=1,
        grid=(tiles,),
        in_specs=[
            pl.BlockSpec((group, TILE, size), lambda t, tb: (0, t, 0)),
            column,
            column,
            lane,
            lane,
            pl.BlockSpec((group * TILE, size), lambda t, tb: (t, 0)),
            pl.BlockSpec(kv_sorted.shape, lambda t, tb: (0, 0)),
        ],
        out_specs=pl.BlockSpec((group, TILE, size), lambda t, tb: (0, t, 0)),
    )
    return pl.pallas_call(
        body,
        grid_spec=spec,
        out_shape=jax.ShapeDtypeStruct(q_sorted.shape, jnp.bfloat16),
        compiler_params=pltpu.CompilerParams(dimension_semantics=("arbitrary",)),
    )(tables, q_sorted, o_sorted.reshape(count, 1), rs_sorted.reshape(count, 1), *state, kv_sorted)


def rotate_columns(value, shift):
    doubled = jnp.concatenate([value, value], axis=1)
    return lax.dynamic_slice_in_dim(doubled, shift, value.shape[1], axis=1)


def gather_heads(piece):
    parts = lax.psum(1, "heads")
    me = lax.axis_index("heads")
    width = piece.shape[1]
    full = jnp.zeros((piece.shape[0], parts * width), piece.dtype)
    for shift in range(parts):
        got = piece
        if shift > 0:
            pairs = [(i, (i + shift) % parts) for i in range(parts)]
            got = lax.ppermute(piece, "heads", pairs)
        source = lax.rem(me - shift + parts, parts)
        full = lax.dynamic_update_slice_in_dim(full, got, source * width, axis=1)
    return full


def scatter_heads(partial_value):
    parts = lax.psum(1, "heads")
    me = lax.axis_index("heads")
    width = partial_value.shape[1] // parts
    ahead = rotate_columns(partial_value.astype(jnp.bfloat16), me * width)
    total = ahead[:, :width].astype(jnp.float32)
    for shift in range(1, parts):
        pairs = [(i, (i + shift) % parts) for i in range(parts)]
        piece = ahead[:, shift * width:(shift + 1) * width]
        total = total + lax.ppermute(piece, "heads", pairs).astype(jnp.float32)
    return total.astype(jnp.bfloat16)


def on_device(
    tokens,
    order,
    lengths,
    block_table,
    destination,
    w_query,
    key_weight,
    value_weight,
    w_out,
    key_value_cache,
):
    local_heads = key_weight.shape[1] // HEAD_SIZE
    layer_zero = key_value_cache[0]
    used = jnp.take(layer_zero, block_table.reshape(-1), axis=0)
    pool, span = used.shape[0], used.shape[1]
    used = used.reshape(pool, span, 2, local_heads, HEAD_SIZE).transpose(0, 1, 3, 2, 4)
    used = used.reshape(pool, span, local_heads * 2 * HEAD_SIZE)
    cache = lax.all_gather(used, "seq", axis=1, tiled=True)
    by_order = jnp.argsort(order)
    full, by_order = lax.optimization_barrier((gather_heads(tokens), by_order))
    rows = full.shape[0]
    wide = full.astype(jnp.float32)
    normed = (wide * lax.rsqrt(jnp.mean(wide * wide, axis=1, keepdims=True) + epsilon)).astype(
        jnp.bfloat16
    )
    local_heads = key_weight.shape[1] // HEAD_SIZE
    head_group = QUERY_HEADS // KEY_VALUE_HEADS
    query_rows = jnp.dot(normed, w_query, preferred_element_type=jnp.float32)
    key_rows = jnp.dot(normed, key_weight, preferred_element_type=jnp.float32)
    value_rows = jnp.dot(normed, value_weight, preferred_element_type=jnp.float32)
    device = lax.axis_index("seq")
    my_order = lax.dynamic_slice_in_dim(order, device * rows, rows)
    request, position = request_place(my_order, lengths)
    rotary_angles = (position + CB * BLOCK_POSITIONS).astype(jnp.float32)
    query_rows = apply_rotary(
        query_rows.reshape(rows, local_heads * head_group, HEAD_SIZE), rotary_angles
    ).astype(jnp.bfloat16)
    query_rows = query_rows.reshape(rows, local_heads, head_group, HEAD_SIZE)
    key_rows = (
        apply_rotary(key_rows.reshape(rows, local_heads, HEAD_SIZE), rotary_angles)
        .astype(jnp.bfloat16)
        .reshape(rows, local_heads * HEAD_SIZE)
    )
    fresh_rows = jnp.concatenate(
        [
            key_rows.reshape(rows, local_heads, HEAD_SIZE),
            value_rows.astype(jnp.bfloat16).reshape(rows, local_heads, HEAD_SIZE),
        ],
        axis=2,
    ).reshape(rows, local_heads * 2 * HEAD_SIZE)
    fresh_rows, cache = lax.optimization_barrier((fresh_rows, cache))
    gathered = lax.all_gather(fresh_rows, "seq", axis=0, tiled=True)
    kv_sorted = jnp.take(gathered, by_order, axis=0)
    earlier = (my_order[None, :] < my_order[:, None]).astype(jnp.int32)
    unsort = jnp.sum(earlier, axis=1)
    slots_of = jnp.arange(rows, dtype=jnp.int32)
    perm = jnp.sum(jnp.where(unsort[:, None] == slots_of[None, :], slots_of[:, None], 0), axis=0)
    o_sorted = jnp.take(my_order, perm)
    rs_sorted = jnp.take(my_order - position, perm)
    req_sorted = jnp.take(request, perm)
    q_sorted = jnp.take(query_rows, perm, axis=0)
    tables = attention_tables(o_sorted, rs_sorted, req_sorted)
    outs = []
    for head in range(local_heads):
        q_head = q_sorted[:, head].transpose(1, 0, 2)
        part = slice(head * 2 * HEAD_SIZE, (head + 1) * 2 * HEAD_SIZE)
        state = cache_attention(tables, q_head, req_sorted, cache[:, :, part])
        result = fresh_attention(tables, q_head, o_sorted, rs_sorted, state, kv_sorted[:, part])
        outs.append(result)
    outs = [jnp.take(result, unsort, axis=1).transpose(1, 0, 2) for result in outs]
    attn = jnp.stack(outs, axis=1).reshape(rows, local_heads * head_group * HEAD_SIZE)
    partial_value = jnp.dot(attn, w_out, preferred_element_type=jnp.float32)
    partial_value, pool_blocks = lax.optimization_barrier((partial_value, key_value_cache))
    slots = destination.shape[0]
    slot_labels = jnp.arange(slots, dtype=jnp.int32)
    inverse = jnp.sum(
        jnp.where(destination[None, :] == slot_labels[:, None], slot_labels[None, :], 0), axis=1
    )
    arranged = jnp.take(pool_blocks, inverse, axis=1)
    decode_cache = lax.all_to_all(arranged, "seq", split_axis=1, concat_axis=2, tiled=True)
    attn_out = scatter_heads(partial_value)
    return (attn_out, decode_cache)


def solution(mesh):
    placed = (
        P("seq", "heads"),
        P(),
        P(),
        P(),
        P(),
        P(None, "heads"),
        P(None, "heads"),
        P(None, "heads"),
        P("heads", None),
        P(None, None, "seq", None, "heads"),
    )
    return jax.shard_map(
        on_device,
        mesh=mesh,
        in_specs=placed,
        out_specs=(P("seq", "heads"), P(None, "seq", None, None, "heads")),
        check_vma=False,
    )
```

```python
import jax
import jax.numpy as jnp
from jax import lax
from jax.sharding import PartitionSpec as P
import functools
from jax.experimental import pallas as pl
from jax.experimental.pallas import tpu as pltpu

QUERY_HEADS = 40
KEY_VALUE_HEADS = 8
HEAD_SIZE = 128
BLOCK_POSITIONS = 512
CB = 2


theta = 1000000.0
epsilon = 1e-06


def apply_rotary(value_rows, place):
    half = value_rows.shape[-1] // 2
    freq = theta ** (-2.0 * jnp.arange(half, dtype=jnp.float32) / value_rows.shape[-1])
    angle = place[:, None, None] * freq
    cosine = jnp.cos(angle)
    sine_part = jnp.sin(angle)
    first = value_rows[..., :half]
    second = value_rows[..., half:]
    return jnp.concatenate(
        [first * cosine - second * sine_part, second * cosine + first * sine_part], axis=-1
    )


def request_place(order, lengths):
    ends = jnp.cumsum(lengths)
    starts = ends - lengths
    request = jnp.sum((order[:, None] >= ends[None, :]).astype(jnp.int32), axis=1)
    labels = jnp.arange(lengths.shape[0], dtype=jnp.int32)
    begin = jnp.sum(jnp.where(request[:, None] == labels[None, :], starts[None, :], 0), axis=1)
    return (request, order - begin)


from jax.experimental import pallas as pl
from jax.experimental.pallas import tpu as pltpu

TILE = 32
CHUNK = 512


def _online(q, keys, values, mask, carry, scale):
    top, total, accum = carry
    width = keys.shape[0]
    scores = lax.dot_general(q, keys, (((1,), (1,)), ((), ())), preferred_element_type=jnp.float32) * scale
    scores = scores.reshape(-1, mask.shape[0], width)
    scores = jnp.where(mask[None], scores, -1e30).reshape(q.shape[0], width)
    new_top = jnp.maximum(top, jnp.max(scores, axis=1, keepdims=True))
    expo = jnp.exp(scores - new_top)
    fade = jnp.exp(top - new_top)
    total = total * fade + jnp.sum(expo, axis=1, keepdims=True)
    accum = accum * fade + jnp.dot(expo.astype(jnp.bfloat16), values, preferred_element_type=jnp.float32)
    return (new_top, total, accum)


def _cache_body(tables, q_ref, req_ref, cache_ref, top_ref, total_ref, accum_ref, *, scale):
    t = pl.program_id(0)
    group, rows, size = q_ref.shape
    q = q_ref[...].reshape(group * rows, size)
    req_row = req_ref[...]

    def cached(r, carry):
        mask = req_row == r
        block = jnp.concatenate([cache_ref[2 * r], cache_ref[2 * r + 1]], axis=0)
        return _online(q, block[:, :size], block[:, size:], mask, carry, scale)

    carry = (
        jnp.full((group * rows, 1), -1e30, jnp.float32),
        jnp.zeros((group * rows, 1), jnp.float32),
        jnp.zeros((group * rows, size), jnp.float32),
    )
    top, total, accum = lax.fori_loop(tables[0, t], tables[1, t] + 1, cached, carry)
    top_ref[...] = top
    total_ref[...] = total
    accum_ref[...] = accum


def _fresh_body(tables, q_ref, o_ref, rs_ref, top_ref, total_ref, accum_ref, kv_ref, out_ref, *, scale):
    t = pl.program_id(0)
    group, rows, size = q_ref.shape
    q = q_ref[...].reshape(group * rows, size)
    o_row = o_ref[...]
    rs_row = rs_ref[...]

    def fresh(c, carry):
        start = pl.multiple_of(c * CHUNK, CHUNK)
        block = kv_ref[pl.ds(start, CHUNK), :]
        index = start + lax.broadcasted_iota(jnp.int32, (1, CHUNK), 1)
        mask = (index >= rs_row) & (index <= o_row)
        return _online(q, block[:, :size], block[:, size:], mask, carry, scale)

    carry = (top_ref[...], total_ref[...], accum_ref[...])
    top, total, accum = lax.fori_loop(tables[2, t], tables[3, t] + 1, fresh, carry)
    out_ref[...] = (accum / total).reshape(group, rows, size).astype(out_ref.dtype)


def attention_tables(o_sorted, rs_sorted, req_sorted):
    count = o_sorted.shape[0]
    firsts = jnp.arange(count // TILE) * TILE
    lasts = firsts + TILE - 1
    return jnp.stack([
        req_sorted[firsts], req_sorted[lasts], rs_sorted[firsts] // CHUNK, o_sorted[lasts] // CHUNK
    ]).astype(jnp.int32)


def cache_attention(tables, q_sorted, req_sorted, cache):
    group, count, size = q_sorted.shape
    tiles = count // TILE
    body = functools.partial(_cache_body, scale=size ** (-0.5))
    state = pl.BlockSpec((group * TILE, 1), lambda t, tb: (t, 0))
    spec = pltpu.PrefetchScalarGridSpec(
        num_scalar_prefetch=1,
        grid=(tiles,),
        in_specs=[
            pl.BlockSpec((group, TILE, size), lambda t, tb: (0, t, 0)),
            pl.BlockSpec((TILE, 1), lambda t, tb: (t, 0)),
            pl.BlockSpec(cache.shape, lambda t, tb: (0, 0, 0)),
        ],
        out_specs=[state, state, pl.BlockSpec((group * TILE, size), lambda t, tb: (t, 0))],
    )
    return pl.pallas_call(
        body,
        grid_spec=spec,
        out_shape=[
            jax.ShapeDtypeStruct((group * count, 1), jnp.float32),
            jax.ShapeDtypeStruct((group * count, 1), jnp.float32),
            jax.ShapeDtypeStruct((group * count, size), jnp.float32),
        ],
        compiler_params=pltpu.CompilerParams(dimension_semantics=("arbitrary",)),
    )(tables, q_sorted, req_sorted.reshape(count, 1), cache)


def fresh_attention(tables, q_sorted, o_sorted, rs_sorted, state, kv_sorted):
    group, count, size = q_sorted.shape
    tiles = count // TILE
    body = functools.partial(_fresh_body, scale=size ** (-0.5))
    column = pl.BlockSpec((TILE, 1), lambda t, tb: (t, 0))
    lane = pl.BlockSpec((group * TILE, 1), lambda t, tb: (t, 0))
    spec = pltpu.PrefetchScalarGridSpec(
        num_scalar_prefetch=1,
        grid=(tiles,),
        in_specs=[
            pl.BlockSpec((group, TILE, size), lambda t, tb: (0, t, 0)),
            column,
            column,
            lane,
            lane,
            pl.BlockSpec((group * TILE, size), lambda t, tb: (t, 0)),
            pl.BlockSpec(kv_sorted.shape, lambda t, tb: (0, 0)),
        ],
        out_specs=pl.BlockSpec((group, TILE, size), lambda t, tb: (0, t, 0)),
    )
    return pl.pallas_call(
        body,
        grid_spec=spec,
        out_shape=jax.ShapeDtypeStruct(q_sorted.shape, jnp.bfloat16),
        compiler_params=pltpu.CompilerParams(dimension_semantics=("arbitrary",)),
    )(tables, q_sorted, o_sorted.reshape(count, 1), rs_sorted.reshape(count, 1), *state, kv_sorted)


def rotate_columns(value, shift):
    doubled = jnp.concatenate([value, value], axis=1)
    return lax.dynamic_slice_in_dim(doubled, shift, value.shape[1], axis=1)


def gather_heads(piece):
    parts = lax.psum(1, "heads")
    me = lax.axis_index("heads")
    width = piece.shape[1]
    full = jnp.zeros((piece.shape[0], parts * width), piece.dtype)
    for shift in range(parts):
        got = piece
        if shift > 0:
            pairs = [(i, (i + shift) % parts) for i in range(parts)]
            got = lax.ppermute(piece, "heads", pairs)
        source = lax.rem(me - shift + parts, parts)
        full = lax.dynamic_update_slice_in_dim(full, got, source * width, axis=1)
    return full


def scatter_heads(partial_value):
    parts = lax.psum(1, "heads")
    me = lax.axis_index("heads")
    width = partial_value.shape[1] // parts
    ahead = rotate_columns(partial_value.astype(jnp.bfloat16), me * width)
    total = ahead[:, :width].astype(jnp.float32)
    for shift in range(1, parts):
        pairs = [(i, (i + shift) % parts) for i in range(parts)]
        piece = ahead[:, shift * width:(shift + 1) * width]
        total = total + lax.ppermute(piece, "heads", pairs).astype(jnp.float32)
    return total.astype(jnp.bfloat16)


def on_device(
    tokens,
    order,
    lengths,
    block_table,
    destination,
    w_query,
    key_weight,
    value_weight,
    w_out,
    key_value_cache,
):
    local_heads = key_weight.shape[1] // HEAD_SIZE
    slots = destination.shape[0]
    slot_labels = jnp.arange(slots, dtype=jnp.int32)
    inverse = jnp.sum(
        jnp.where(destination[None, :] == slot_labels[:, None], slot_labels[None, :], 0), axis=1
    )
    arranged = jnp.take(key_value_cache, inverse, axis=1)
    layer_zero = key_value_cache[0]
    used = jnp.take(layer_zero, block_table.reshape(-1), axis=0)
    pool, span = used.shape[0], used.shape[1]
    used = used.reshape(pool, span, 2, local_heads, HEAD_SIZE).transpose(0, 1, 3, 2, 4)
    used = used.reshape(pool, span, local_heads * 2 * HEAD_SIZE)
    cache = lax.all_gather(used, "seq", axis=1, tiled=True)
    by_order = jnp.argsort(order)
    full, arranged, by_order = lax.optimization_barrier((gather_heads(tokens), arranged, by_order))
    rows = full.shape[0]
    wide = full.astype(jnp.float32)
    normed = (wide * lax.rsqrt(jnp.mean(wide * wide, axis=1, keepdims=True) + epsilon)).astype(
        jnp.bfloat16
    )
    local_heads = key_weight.shape[1] // HEAD_SIZE
    head_group = QUERY_HEADS // KEY_VALUE_HEADS
    query_rows = jnp.dot(normed, w_query, preferred_element_type=jnp.float32)
    key_rows = jnp.dot(normed, key_weight, preferred_element_type=jnp.float32)
    value_rows = jnp.dot(normed, value_weight, preferred_element_type=jnp.float32)
    device = lax.axis_index("seq")
    my_order = lax.dynamic_slice_in_dim(order, device * rows, rows)
    request, position = request_place(my_order, lengths)
    rotary_angles = (position + CB * BLOCK_POSITIONS).astype(jnp.float32)
    query_rows = apply_rotary(
        query_rows.reshape(rows, local_heads * head_group, HEAD_SIZE), rotary_angles
    ).astype(jnp.bfloat16)
    query_rows = query_rows.reshape(rows, local_heads, head_group, HEAD_SIZE)
    key_rows = (
        apply_rotary(key_rows.reshape(rows, local_heads, HEAD_SIZE), rotary_angles)
        .astype(jnp.bfloat16)
        .reshape(rows, local_heads * HEAD_SIZE)
    )
    fresh_rows = jnp.concatenate(
        [
            key_rows.reshape(rows, local_heads, HEAD_SIZE),
            value_rows.astype(jnp.bfloat16).reshape(rows, local_heads, HEAD_SIZE),
        ],
        axis=2,
    ).reshape(rows, local_heads * 2 * HEAD_SIZE)
    fresh_rows = fresh_rows + jnp.zeros_like(fresh_rows) * cache[0, 0, 0]
    gathered = lax.all_gather(fresh_rows, "seq", axis=0, tiled=True)
    gathered, arranged = lax.optimization_barrier((gathered, arranged))
    decode_cache = lax.all_to_all(arranged, "seq", split_axis=1, concat_axis=2, tiled=True)
    kv_sorted = jnp.take(gathered, by_order, axis=0)
    earlier = (my_order[None, :] < my_order[:, None]).astype(jnp.int32)
    unsort = jnp.sum(earlier, axis=1)
    slots_of = jnp.arange(rows, dtype=jnp.int32)
    perm = jnp.sum(jnp.where(unsort[:, None] == slots_of[None, :], slots_of[:, None], 0), axis=0)
    o_sorted = jnp.take(my_order, perm)
    rs_sorted = jnp.take(my_order - position, perm)
    req_sorted = jnp.take(request, perm)
    q_sorted = jnp.take(query_rows, perm, axis=0)
    tables = attention_tables(o_sorted, rs_sorted, req_sorted)
    outs = []
    for head in range(local_heads):
        q_head = q_sorted[:, head].transpose(1, 0, 2)
        part = slice(head * 2 * HEAD_SIZE, (head + 1) * 2 * HEAD_SIZE)
        state = cache_attention(tables, q_head, req_sorted, cache[:, :, part])
        result = fresh_attention(tables, q_head, o_sorted, rs_sorted, state, kv_sorted[:, part])
        outs.append(result)
    outs = [jnp.take(result, unsort, axis=1).transpose(1, 0, 2) for result in outs]
    attn = jnp.stack(outs, axis=1).reshape(rows, local_heads * head_group * HEAD_SIZE)
    partial_value = jnp.dot(attn, w_out, preferred_element_type=jnp.float32)
    attn_out = scatter_heads(partial_value)
    return (attn_out, decode_cache)


def solution(mesh):
    placed = (
        P("seq", "heads"),
        P(),
        P(),
        P(),
        P(),
        P(None, "heads"),
        P(None, "heads"),
        P(None, "heads"),
        P("heads", None),
        P(None, None, "seq", None, "heads"),
    )
    return jax.shard_map(
        on_device,
        mesh=mesh,
        in_specs=placed,
        out_specs=(P("seq", "heads"), P(None, "seq", None, None, "heads")),
        check_vma=False,
    )
```

```python
import jax
import jax.numpy as jnp
from jax import lax
from jax.sharding import PartitionSpec as P
import functools
from jax.experimental import pallas as pl
from jax.experimental.pallas import tpu as pltpu

QUERY_HEADS = 40
KEY_VALUE_HEADS = 8
HEAD_SIZE = 128
BLOCK_POSITIONS = 512
CB = 2


theta = 1000000.0
epsilon = 1e-06


def apply_rotary(value_rows, place):
    half = value_rows.shape[-1] // 2
    freq = theta ** (-2.0 * jnp.arange(half, dtype=jnp.float32) / value_rows.shape[-1])
    angle = place[:, None, None] * freq
    cosine = jnp.cos(angle)
    sine_part = jnp.sin(angle)
    first = value_rows[..., :half]
    second = value_rows[..., half:]
    return jnp.concatenate(
        [first * cosine - second * sine_part, second * cosine + first * sine_part], axis=-1
    )


def request_place(order, lengths):
    ends = jnp.cumsum(lengths)
    starts = ends - lengths
    request = jnp.sum((order[:, None] >= ends[None, :]).astype(jnp.int32), axis=1)
    labels = jnp.arange(lengths.shape[0], dtype=jnp.int32)
    begin = jnp.sum(jnp.where(request[:, None] == labels[None, :], starts[None, :], 0), axis=1)
    return (request, order - begin)


from jax.experimental import pallas as pl
from jax.experimental.pallas import tpu as pltpu

TILE = 32
CHUNK = 512


def _online(q, keys, values, mask, carry, scale):
    top, total, accum = carry
    width = keys.shape[0]
    scores = lax.dot_general(q, keys, (((1,), (1,)), ((), ())), preferred_element_type=jnp.float32) * scale
    scores = scores.reshape(-1, mask.shape[0], width)
    scores = jnp.where(mask[None], scores, -1e30).reshape(q.shape[0], width)
    new_top = jnp.maximum(top, jnp.max(scores, axis=1, keepdims=True))
    expo = jnp.exp(scores - new_top)
    fade = jnp.exp(top - new_top)
    total = total * fade + jnp.sum(expo, axis=1, keepdims=True)
    accum = accum * fade + jnp.dot(expo.astype(jnp.bfloat16), values, preferred_element_type=jnp.float32)
    return (new_top, total, accum)


def _cache_body(tables, q_ref, req_ref, cache_ref, top_ref, total_ref, accum_ref, *, scale):
    t = pl.program_id(0)
    group, rows, size = q_ref.shape
    q = q_ref[...].reshape(group * rows, size)
    req_row = req_ref[...]

    def cached(r, carry):
        mask = req_row == r
        block = jnp.concatenate([cache_ref[2 * r], cache_ref[2 * r + 1]], axis=0)
        return _online(q, block[:, :size], block[:, size:], mask, carry, scale)

    carry = (
        jnp.full((group * rows, 1), -1e30, jnp.float32),
        jnp.zeros((group * rows, 1), jnp.float32),
        jnp.zeros((group * rows, size), jnp.float32),
    )
    top, total, accum = lax.fori_loop(tables[0, t], tables[1, t] + 1, cached, carry)
    top_ref[...] = top
    total_ref[...] = total
    accum_ref[...] = accum


def _fresh_body(tables, q_ref, o_ref, rs_ref, top_ref, total_ref, accum_ref, kv_ref, out_ref, *, scale):
    t = pl.program_id(0)
    group, rows, size = q_ref.shape
    q = q_ref[...].reshape(group * rows, size)
    o_row = o_ref[...]
    rs_row = rs_ref[...]

    def fresh(c, carry):
        start = pl.multiple_of(c * CHUNK, CHUNK)
        block = kv_ref[pl.ds(start, CHUNK), :]
        index = start + lax.broadcasted_iota(jnp.int32, (1, CHUNK), 1)
        mask = (index >= rs_row) & (index <= o_row)
        return _online(q, block[:, :size], block[:, size:], mask, carry, scale)

    carry = (top_ref[...], total_ref[...], accum_ref[...])
    top, total, accum = lax.fori_loop(tables[2, t], tables[3, t] + 1, fresh, carry)
    out_ref[...] = (accum / total).reshape(group, rows, size).astype(out_ref.dtype)


def attention_tables(o_sorted, rs_sorted, req_sorted):
    count = o_sorted.shape[0]
    firsts = jnp.arange(count // TILE) * TILE
    lasts = firsts + TILE - 1
    return jnp.stack([
        req_sorted[firsts], req_sorted[lasts], rs_sorted[firsts] // CHUNK, o_sorted[lasts] // CHUNK
    ]).astype(jnp.int32)


def cache_attention(tables, q_sorted, req_sorted, cache):
    group, count, size = q_sorted.shape
    tiles = count // TILE
    body = functools.partial(_cache_body, scale=size ** (-0.5))
    state = pl.BlockSpec((group * TILE, 1), lambda t, tb: (t, 0))
    spec = pltpu.PrefetchScalarGridSpec(
        num_scalar_prefetch=1,
        grid=(tiles,),
        in_specs=[
            pl.BlockSpec((group, TILE, size), lambda t, tb: (0, t, 0)),
            pl.BlockSpec((TILE, 1), lambda t, tb: (t, 0)),
            pl.BlockSpec(cache.shape, lambda t, tb: (0, 0, 0)),
        ],
        out_specs=[state, state, pl.BlockSpec((group * TILE, size), lambda t, tb: (t, 0))],
    )
    return pl.pallas_call(
        body,
        grid_spec=spec,
        out_shape=[
            jax.ShapeDtypeStruct((group * count, 1), jnp.float32),
            jax.ShapeDtypeStruct((group * count, 1), jnp.float32),
            jax.ShapeDtypeStruct((group * count, size), jnp.float32),
        ],
        compiler_params=pltpu.CompilerParams(dimension_semantics=("arbitrary",)),
    )(tables, q_sorted, req_sorted.reshape(count, 1), cache)


def fresh_attention(tables, q_sorted, o_sorted, rs_sorted, state, kv_sorted):
    group, count, size = q_sorted.shape
    tiles = count // TILE
    body = functools.partial(_fresh_body, scale=size ** (-0.5))
    column = pl.BlockSpec((TILE, 1), lambda t, tb: (t, 0))
    lane = pl.BlockSpec((group * TILE, 1), lambda t, tb: (t, 0))
    spec = pltpu.PrefetchScalarGridSpec(
        num_scalar_prefetch=1,
        grid=(tiles,),
        in_specs=[
            pl.BlockSpec((group, TILE, size), lambda t, tb: (0, t, 0)),
            column,
            column,
            lane,
            lane,
            pl.BlockSpec((group * TILE, size), lambda t, tb: (t, 0)),
            pl.BlockSpec(kv_sorted.shape, lambda t, tb: (0, 0)),
        ],
        out_specs=pl.BlockSpec((group, TILE, size), lambda t, tb: (0, t, 0)),
    )
    return pl.pallas_call(
        body,
        grid_spec=spec,
        out_shape=jax.ShapeDtypeStruct(q_sorted.shape, jnp.bfloat16),
        compiler_params=pltpu.CompilerParams(dimension_semantics=("arbitrary",)),
    )(tables, q_sorted, o_sorted.reshape(count, 1), rs_sorted.reshape(count, 1), *state, kv_sorted)


def rotate_columns(value, shift):
    doubled = jnp.concatenate([value, value], axis=1)
    return lax.dynamic_slice_in_dim(doubled, shift, value.shape[1], axis=1)


def gather_heads(piece):
    parts = lax.psum(1, "heads")
    me = lax.axis_index("heads")
    width = piece.shape[1]
    full = jnp.zeros((piece.shape[0], parts * width), piece.dtype)
    for shift in range(parts):
        got = piece
        if shift > 0:
            pairs = [(i, (i + shift) % parts) for i in range(parts)]
            got = lax.ppermute(piece, "heads", pairs)
        source = lax.rem(me - shift + parts, parts)
        full = lax.dynamic_update_slice_in_dim(full, got, source * width, axis=1)
    return full


def scatter_heads(partial_value):
    parts = lax.psum(1, "heads")
    me = lax.axis_index("heads")
    width = partial_value.shape[1] // parts
    ahead = rotate_columns(partial_value.astype(jnp.bfloat16), me * width)
    total = ahead[:, :width].astype(jnp.float32)
    for shift in range(1, parts):
        pairs = [(i, (i + shift) % parts) for i in range(parts)]
        piece = ahead[:, shift * width:(shift + 1) * width]
        total = total + lax.ppermute(piece, "heads", pairs).astype(jnp.float32)
    return total.astype(jnp.bfloat16)


def on_device(
    tokens,
    order,
    lengths,
    block_table,
    destination,
    w_query,
    key_weight,
    value_weight,
    w_out,
    key_value_cache,
):
    local_heads = key_weight.shape[1] // HEAD_SIZE
    slots = destination.shape[0]
    slot_labels = jnp.arange(slots, dtype=jnp.int32)
    inverse = jnp.sum(
        jnp.where(destination[None, :] == slot_labels[:, None], slot_labels[None, :], 0), axis=1
    )
    arranged = jnp.take(key_value_cache, inverse, axis=1)
    layer_zero = key_value_cache[0]
    used = jnp.take(layer_zero, block_table.reshape(-1), axis=0)
    pool, span = used.shape[0], used.shape[1]
    used = used.reshape(pool, span, 2, local_heads, HEAD_SIZE).transpose(0, 1, 3, 2, 4)
    used = used.reshape(pool, span, local_heads * 2 * HEAD_SIZE)
    cache = lax.all_gather(used, "seq", axis=1, tiled=True)
    by_order = jnp.argsort(order)
    full, arranged, by_order = lax.optimization_barrier((gather_heads(tokens), arranged, by_order))
    rows = full.shape[0]
    wide = full.astype(jnp.float32)
    normed = (wide * lax.rsqrt(jnp.mean(wide * wide, axis=1, keepdims=True) + epsilon)).astype(
        jnp.bfloat16
    )
    local_heads = key_weight.shape[1] // HEAD_SIZE
    head_group = QUERY_HEADS // KEY_VALUE_HEADS
    query_rows = jnp.dot(normed, w_query, preferred_element_type=jnp.float32)
    key_rows = jnp.dot(normed, key_weight, preferred_element_type=jnp.float32)
    value_rows = jnp.dot(normed, value_weight, preferred_element_type=jnp.float32)
    device = lax.axis_index("seq")
    my_order = lax.dynamic_slice_in_dim(order, device * rows, rows)
    request, position = request_place(my_order, lengths)
    rotary_angles = (position + CB * BLOCK_POSITIONS).astype(jnp.float32)
    query_rows = apply_rotary(
        query_rows.reshape(rows, local_heads * head_group, HEAD_SIZE), rotary_angles
    ).astype(jnp.bfloat16)
    query_rows = query_rows.reshape(rows, local_heads, head_group, HEAD_SIZE)
    key_rows = (
        apply_rotary(key_rows.reshape(rows, local_heads, HEAD_SIZE), rotary_angles)
        .astype(jnp.bfloat16)
        .reshape(rows, local_heads * HEAD_SIZE)
    )
    fresh_rows = jnp.concatenate(
        [
            key_rows.reshape(rows, local_heads, HEAD_SIZE),
            value_rows.astype(jnp.bfloat16).reshape(rows, local_heads, HEAD_SIZE),
        ],
        axis=2,
    ).reshape(rows, local_heads * 2 * HEAD_SIZE)
    peers = lax.psum(1, "seq")
    spread = jnp.broadcast_to(fresh_rows[None], (peers,) + fresh_rows.shape)
    gathered = lax.all_to_all(spread, "seq", 0, 0, tiled=True).reshape(peers * rows, fresh_rows.shape[1])
    gathered, arranged = lax.optimization_barrier((gathered, arranged))
    decode_cache = lax.all_to_all(arranged, "seq", split_axis=1, concat_axis=2, tiled=True)
    kv_sorted = jnp.take(gathered, by_order, axis=0)
    earlier = (my_order[None, :] < my_order[:, None]).astype(jnp.int32)
    unsort = jnp.sum(earlier, axis=1)
    slots_of = jnp.arange(rows, dtype=jnp.int32)
    perm = jnp.sum(jnp.where(unsort[:, None] == slots_of[None, :], slots_of[:, None], 0), axis=0)
    o_sorted = jnp.take(my_order, perm)
    rs_sorted = jnp.take(my_order - position, perm)
    req_sorted = jnp.take(request, perm)
    q_sorted = jnp.take(query_rows, perm, axis=0)
    tables = attention_tables(o_sorted, rs_sorted, req_sorted)
    outs = []
    for head in range(local_heads):
        q_head = q_sorted[:, head].transpose(1, 0, 2)
        part = slice(head * 2 * HEAD_SIZE, (head + 1) * 2 * HEAD_SIZE)
        state = cache_attention(tables, q_head, req_sorted, cache[:, :, part])
        result = fresh_attention(tables, q_head, o_sorted, rs_sorted, state, kv_sorted[:, part])
        outs.append(result)
    outs = [jnp.take(result, unsort, axis=1).transpose(1, 0, 2) for result in outs]
    attn = jnp.stack(outs, axis=1).reshape(rows, local_heads * head_group * HEAD_SIZE)
    partial_value = jnp.dot(attn, w_out, preferred_element_type=jnp.float32)
    attn_out = scatter_heads(partial_value)
    return (attn_out, decode_cache)


def solution(mesh):
    placed = (
        P("seq", "heads"),
        P(),
        P(),
        P(),
        P(),
        P(None, "heads"),
        P(None, "heads"),
        P(None, "heads"),
        P("heads", None),
        P(None, None, "seq", None, "heads"),
    )
    return jax.shard_map(
        on_device,
        mesh=mesh,
        in_specs=placed,
        out_specs=(P("seq", "heads"), P(None, "seq", None, None, "heads")),
        check_vma=False,
    )
```

```python
import jax
import jax.numpy as jnp
from jax import lax
from jax.sharding import PartitionSpec as P
import functools
from jax.experimental import pallas as pl
from jax.experimental.pallas import tpu as pltpu

QUERY_HEADS = 40
KEY_VALUE_HEADS = 8
HEAD_SIZE = 128
BLOCK_POSITIONS = 512
CB = 2


theta = 1000000.0
epsilon = 1e-06


def apply_rotary(value_rows, place):
    half = value_rows.shape[-1] // 2
    freq = theta ** (-2.0 * jnp.arange(half, dtype=jnp.float32) / value_rows.shape[-1])
    angle = place[:, None, None] * freq
    cosine = jnp.cos(angle)
    sine_part = jnp.sin(angle)
    first = value_rows[..., :half]
    second = value_rows[..., half:]
    return jnp.concatenate(
        [first * cosine - second * sine_part, second * cosine + first * sine_part], axis=-1
    )


def request_place(order, lengths):
    ends = jnp.cumsum(lengths)
    starts = ends - lengths
    request = jnp.sum((order[:, None] >= ends[None, :]).astype(jnp.int32), axis=1)
    labels = jnp.arange(lengths.shape[0], dtype=jnp.int32)
    begin = jnp.sum(jnp.where(request[:, None] == labels[None, :], starts[None, :], 0), axis=1)
    return (request, order - begin)


from jax.experimental import pallas as pl
from jax.experimental.pallas import tpu as pltpu

TILE = 32
CHUNK = 1024


def _online(q, keys, values, mask, carry, scale):
    top, total, accum = carry
    width = keys.shape[0]
    scores = lax.dot_general(q, keys, (((1,), (1,)), ((), ())), preferred_element_type=jnp.float32) * scale
    scores = scores.reshape(-1, mask.shape[0], width)
    scores = jnp.where(mask[None], scores, -1e30).reshape(q.shape[0], width)
    new_top = jnp.maximum(top, jnp.max(scores, axis=1, keepdims=True))
    expo = jnp.exp(scores - new_top)
    fade = jnp.exp(top - new_top)
    total = total * fade + jnp.sum(expo, axis=1, keepdims=True)
    accum = accum * fade + jnp.dot(expo.astype(jnp.bfloat16), values, preferred_element_type=jnp.float32)
    return (new_top, total, accum)


def _cache_body(tables, q_ref, req_ref, cache_ref, top_ref, total_ref, accum_ref, *, scale):
    t = pl.program_id(0)
    group, rows, size = q_ref.shape
    q = q_ref[...].reshape(group * rows, size)
    req_row = req_ref[...]

    def cached(r, carry):
        mask = req_row == r
        block = jnp.concatenate([cache_ref[2 * r], cache_ref[2 * r + 1]], axis=0)
        return _online(q, block[:, :size], block[:, size:], mask, carry, scale)

    carry = (
        jnp.full((group * rows, 1), -1e30, jnp.float32),
        jnp.zeros((group * rows, 1), jnp.float32),
        jnp.zeros((group * rows, size), jnp.float32),
    )
    top, total, accum = lax.fori_loop(tables[0, t], tables[1, t] + 1, cached, carry)
    top_ref[...] = top
    total_ref[...] = total
    accum_ref[...] = accum


def _fresh_body(tables, q_ref, o_ref, rs_ref, top_ref, total_ref, accum_ref, kv_ref, out_ref, *, scale):
    t = pl.program_id(0)
    group, rows, size = q_ref.shape
    q = q_ref[...].reshape(group * rows, size)
    o_row = o_ref[...]
    rs_row = rs_ref[...]

    def fresh(c, carry):
        start = pl.multiple_of(c * CHUNK, CHUNK)
        block = kv_ref[pl.ds(start, CHUNK), :]
        index = start + lax.broadcasted_iota(jnp.int32, (1, CHUNK), 1)
        mask = (index >= rs_row) & (index <= o_row)
        return _online(q, block[:, :size], block[:, size:], mask, carry, scale)

    carry = (top_ref[...], total_ref[...], accum_ref[...])
    top, total, accum = lax.fori_loop(tables[2, t], tables[3, t] + 1, fresh, carry)
    out_ref[...] = (accum / total).reshape(group, rows, size).astype(out_ref.dtype)


def attention_tables(o_sorted, rs_sorted, req_sorted):
    count = o_sorted.shape[0]
    firsts = jnp.arange(count // TILE) * TILE
    lasts = firsts + TILE - 1
    return jnp.stack([
        req_sorted[firsts], req_sorted[lasts], rs_sorted[firsts] // CHUNK, o_sorted[lasts] // CHUNK
    ]).astype(jnp.int32)


def cache_attention(tables, q_sorted, req_sorted, cache):
    group, count, size = q_sorted.shape
    tiles = count // TILE
    body = functools.partial(_cache_body, scale=size ** (-0.5))
    state = pl.BlockSpec((group * TILE, 1), lambda t, tb: (t, 0))
    spec = pltpu.PrefetchScalarGridSpec(
        num_scalar_prefetch=1,
        grid=(tiles,),
        in_specs=[
            pl.BlockSpec((group, TILE, size), lambda t, tb: (0, t, 0)),
            pl.BlockSpec((TILE, 1), lambda t, tb: (t, 0)),
            pl.BlockSpec(cache.shape, lambda t, tb: (0, 0, 0)),
        ],
        out_specs=[state, state, pl.BlockSpec((group * TILE, size), lambda t, tb: (t, 0))],
    )
    return pl.pallas_call(
        body,
        grid_spec=spec,
        out_shape=[
            jax.ShapeDtypeStruct((group * count, 1), jnp.float32),
            jax.ShapeDtypeStruct((group * count, 1), jnp.float32),
            jax.ShapeDtypeStruct((group * count, size), jnp.float32),
        ],
        compiler_params=pltpu.CompilerParams(dimension_semantics=("arbitrary",)),
    )(tables, q_sorted, req_sorted.reshape(count, 1), cache)


def fresh_attention(tables, q_sorted, o_sorted, rs_sorted, state, kv_sorted):
    group, count, size = q_sorted.shape
    tiles = count // TILE
    body = functools.partial(_fresh_body, scale=size ** (-0.5))
    column = pl.BlockSpec((TILE, 1), lambda t, tb: (t, 0))
    lane = pl.BlockSpec((group * TILE, 1), lambda t, tb: (t, 0))
    spec = pltpu.PrefetchScalarGridSpec(
        num_scalar_prefetch=1,
        grid=(tiles,),
        in_specs=[
            pl.BlockSpec((group, TILE, size), lambda t, tb: (0, t, 0)),
            column,
            column,
            lane,
            lane,
            pl.BlockSpec((group * TILE, size), lambda t, tb: (t, 0)),
            pl.BlockSpec(kv_sorted.shape, lambda t, tb: (0, 0)),
        ],
        out_specs=pl.BlockSpec((group, TILE, size), lambda t, tb: (0, t, 0)),
    )
    return pl.pallas_call(
        body,
        grid_spec=spec,
        out_shape=jax.ShapeDtypeStruct(q_sorted.shape, jnp.bfloat16),
        compiler_params=pltpu.CompilerParams(dimension_semantics=("arbitrary",)),
    )(tables, q_sorted, o_sorted.reshape(count, 1), rs_sorted.reshape(count, 1), *state, kv_sorted)


def rotate_columns(value, shift):
    doubled = jnp.concatenate([value, value], axis=1)
    return lax.dynamic_slice_in_dim(doubled, shift, value.shape[1], axis=1)


def gather_heads(piece):
    parts = lax.psum(1, "heads")
    me = lax.axis_index("heads")
    width = piece.shape[1]
    full = jnp.zeros((piece.shape[0], parts * width), piece.dtype)
    for shift in range(parts):
        got = piece
        if shift > 0:
            pairs = [(i, (i + shift) % parts) for i in range(parts)]
            got = lax.ppermute(piece, "heads", pairs)
        source = lax.rem(me - shift + parts, parts)
        full = lax.dynamic_update_slice_in_dim(full, got, source * width, axis=1)
    return full


def scatter_heads(partial_value):
    parts = lax.psum(1, "heads")
    me = lax.axis_index("heads")
    width = partial_value.shape[1] // parts
    ahead = rotate_columns(partial_value.astype(jnp.bfloat16), me * width)
    total = ahead[:, :width].astype(jnp.float32)
    for shift in range(1, parts):
        pairs = [(i, (i + shift) % parts) for i in range(parts)]
        piece = ahead[:, shift * width:(shift + 1) * width]
        total = total + lax.ppermute(piece, "heads", pairs).astype(jnp.float32)
    return total.astype(jnp.bfloat16)


def on_device(
    tokens,
    order,
    lengths,
    block_table,
    destination,
    w_query,
    key_weight,
    value_weight,
    w_out,
    key_value_cache,
):
    local_heads = key_weight.shape[1] // HEAD_SIZE
    slots = destination.shape[0]
    slot_labels = jnp.arange(slots, dtype=jnp.int32)
    inverse = jnp.sum(
        jnp.where(destination[None, :] == slot_labels[:, None], slot_labels[None, :], 0), axis=1
    )
    arranged = jnp.take(key_value_cache, inverse, axis=1)
    layer_zero = key_value_cache[0]
    used = jnp.take(layer_zero, block_table.reshape(-1), axis=0)
    pool, span = used.shape[0], used.shape[1]
    used = used.reshape(pool, span, 2, local_heads, HEAD_SIZE).transpose(0, 1, 3, 2, 4)
    used = used.reshape(pool, span, local_heads * 2 * HEAD_SIZE)
    cache = lax.all_gather(used, "seq", axis=1, tiled=True)
    by_order = jnp.argsort(order)
    full, arranged, by_order = lax.optimization_barrier((gather_heads(tokens), arranged, by_order))
    rows = full.shape[0]
    wide = full.astype(jnp.float32)
    normed = (wide * lax.rsqrt(jnp.mean(wide * wide, axis=1, keepdims=True) + epsilon)).astype(
        jnp.bfloat16
    )
    local_heads = key_weight.shape[1] // HEAD_SIZE
    head_group = QUERY_HEADS // KEY_VALUE_HEADS
    query_rows = jnp.dot(normed, w_query, preferred_element_type=jnp.float32)
    key_rows = jnp.dot(normed, key_weight, preferred_element_type=jnp.float32)
    value_rows = jnp.dot(normed, value_weight, preferred_element_type=jnp.float32)
    device = lax.axis_index("seq")
    my_order = lax.dynamic_slice_in_dim(order, device * rows, rows)
    request, position = request_place(my_order, lengths)
    rotary_angles = (position + CB * BLOCK_POSITIONS).astype(jnp.float32)
    query_rows = apply_rotary(
        query_rows.reshape(rows, local_heads * head_group, HEAD_SIZE), rotary_angles
    ).astype(jnp.bfloat16)
    query_rows = query_rows.reshape(rows, local_heads, head_group, HEAD_SIZE)
    key_rows = (
        apply_rotary(key_rows.reshape(rows, local_heads, HEAD_SIZE), rotary_angles)
        .astype(jnp.bfloat16)
        .reshape(rows, local_heads * HEAD_SIZE)
    )
    fresh_rows = jnp.concatenate(
        [
            key_rows.reshape(rows, local_heads, HEAD_SIZE),
            value_rows.astype(jnp.bfloat16).reshape(rows, local_heads, HEAD_SIZE),
        ],
        axis=2,
    ).reshape(rows, local_heads * 2 * HEAD_SIZE)
    peers = lax.psum(1, "seq")
    spread = jnp.broadcast_to(fresh_rows[None], (peers,) + fresh_rows.shape)
    gathered = lax.all_to_all(spread, "seq", 0, 0, tiled=True).reshape(peers * rows, fresh_rows.shape[1])
    gathered, arranged = lax.optimization_barrier((gathered, arranged))
    decode_cache = lax.all_to_all(arranged, "seq", split_axis=1, concat_axis=2, tiled=True)
    kv_sorted = jnp.take(gathered, by_order, axis=0)
    earlier = (my_order[None, :] < my_order[:, None]).astype(jnp.int32)
    unsort = jnp.sum(earlier, axis=1)
    slots_of = jnp.arange(rows, dtype=jnp.int32)
    perm = jnp.sum(jnp.where(unsort[:, None] == slots_of[None, :], slots_of[:, None], 0), axis=0)
    o_sorted = jnp.take(my_order, perm)
    rs_sorted = jnp.take(my_order - position, perm)
    req_sorted = jnp.take(request, perm)
    q_sorted = jnp.take(query_rows, perm, axis=0)
    tables = attention_tables(o_sorted, rs_sorted, req_sorted)
    outs = []
    for head in range(local_heads):
        q_head = q_sorted[:, head].transpose(1, 0, 2)
        part = slice(head * 2 * HEAD_SIZE, (head + 1) * 2 * HEAD_SIZE)
        state = cache_attention(tables, q_head, req_sorted, cache[:, :, part])
        result = fresh_attention(tables, q_head, o_sorted, rs_sorted, state, kv_sorted[:, part])
        outs.append(result)
    outs = [jnp.take(result, unsort, axis=1).transpose(1, 0, 2) for result in outs]
    attn = jnp.stack(outs, axis=1).reshape(rows, local_heads * head_group * HEAD_SIZE)
    partial_value = jnp.dot(attn, w_out, preferred_element_type=jnp.float32)
    attn_out = scatter_heads(partial_value)
    return (attn_out, decode_cache)


def solution(mesh):
    placed = (
        P("seq", "heads"),
        P(),
        P(),
        P(),
        P(),
        P(None, "heads"),
        P(None, "heads"),
        P(None, "heads"),
        P("heads", None),
        P(None, None, "seq", None, "heads"),
    )
    return jax.shard_map(
        on_device,
        mesh=mesh,
        in_specs=placed,
        out_specs=(P("seq", "heads"), P(None, "seq", None, None, "heads")),
        check_vma=False,
    )
```

```python
import jax
import jax.numpy as jnp
from jax import lax
from jax.sharding import PartitionSpec as P
import functools
from jax.experimental import pallas as pl
from jax.experimental.pallas import tpu as pltpu

QUERY_HEADS = 40
KEY_VALUE_HEADS = 8
HEAD_SIZE = 128
BLOCK_POSITIONS = 512
CB = 2


theta = 1000000.0
epsilon = 1e-06


def apply_rotary(value_rows, place):
    half = value_rows.shape[-1] // 2
    freq = theta ** (-2.0 * jnp.arange(half, dtype=jnp.float32) / value_rows.shape[-1])
    angle = place[:, None, None] * freq
    cosine = jnp.cos(angle)
    sine_part = jnp.sin(angle)
    first = value_rows[..., :half]
    second = value_rows[..., half:]
    return jnp.concatenate(
        [first * cosine - second * sine_part, second * cosine + first * sine_part], axis=-1
    )


def request_place(order, lengths):
    ends = jnp.cumsum(lengths)
    starts = ends - lengths
    request = jnp.sum((order[:, None] >= ends[None, :]).astype(jnp.int32), axis=1)
    labels = jnp.arange(lengths.shape[0], dtype=jnp.int32)
    begin = jnp.sum(jnp.where(request[:, None] == labels[None, :], starts[None, :], 0), axis=1)
    return (request, order - begin)


from jax.experimental import pallas as pl
from jax.experimental.pallas import tpu as pltpu

TILE = 32
CHUNK = 1024


def _online(q, keys, values, mask, carry, scale):
    top, total, accum = carry
    width = keys.shape[0]
    scores = lax.dot_general(q, keys, (((1,), (1,)), ((), ())), preferred_element_type=jnp.float32) * scale
    scores = scores.reshape(-1, mask.shape[0], width)
    scores = jnp.where(mask[None], scores, -1e30).reshape(q.shape[0], width)
    new_top = jnp.maximum(top, jnp.max(scores, axis=1, keepdims=True))
    expo = jnp.exp(scores - new_top)
    fade = jnp.exp(top - new_top)
    total = total * fade + jnp.sum(expo, axis=1, keepdims=True)
    accum = accum * fade + jnp.dot(expo.astype(jnp.bfloat16), values, preferred_element_type=jnp.float32)
    return (new_top, total, accum)


def _cache_body(tables, q_ref, req_ref, cache_ref, top_ref, total_ref, accum_ref, *, scale):
    t = pl.program_id(0)
    group, rows, size = q_ref.shape
    q = q_ref[...].reshape(group * rows, size)
    req_row = req_ref[...]

    def cached(r, carry):
        mask = req_row == r
        block = jnp.concatenate([cache_ref[2 * r], cache_ref[2 * r + 1]], axis=0)
        return _online(q, block[:, :size], block[:, size:], mask, carry, scale)

    carry = (
        jnp.full((group * rows, 1), -1e30, jnp.float32),
        jnp.zeros((group * rows, 1), jnp.float32),
        jnp.zeros((group * rows, size), jnp.float32),
    )
    top, total, accum = lax.fori_loop(tables[0, t], tables[1, t] + 1, cached, carry)
    top_ref[...] = top
    total_ref[...] = total
    accum_ref[...] = accum


def _fresh_body(tables, q_ref, o_ref, rs_ref, top_ref, total_ref, accum_ref, kv_ref, out_ref, *, scale):
    t = pl.program_id(0)
    group, rows, size = q_ref.shape
    q = q_ref[...].reshape(group * rows, size)
    o_row = o_ref[...]
    rs_row = rs_ref[...]

    def fresh(c, carry):
        start = pl.multiple_of(c * CHUNK, CHUNK)
        block = kv_ref[pl.ds(start, CHUNK), :]
        index = start + lax.broadcasted_iota(jnp.int32, (1, CHUNK), 1)
        mask = (index >= rs_row) & (index <= o_row)
        return _online(q, block[:, :size], block[:, size:], mask, carry, scale)

    carry = (top_ref[...], total_ref[...], accum_ref[...])
    top, total, accum = lax.fori_loop(tables[2, t], tables[3, t] + 1, fresh, carry)
    out_ref[...] = (accum / total).reshape(group, rows, size).astype(out_ref.dtype)


def attention_tables(o_sorted, rs_sorted, req_sorted):
    count = o_sorted.shape[0]
    firsts = jnp.arange(count // TILE) * TILE
    lasts = firsts + TILE - 1
    return jnp.stack([
        req_sorted[firsts], req_sorted[lasts], rs_sorted[firsts] // CHUNK, o_sorted[lasts] // CHUNK
    ]).astype(jnp.int32)


def cache_attention(tables, q_sorted, req_sorted, cache):
    group, count, size = q_sorted.shape
    tiles = count // TILE
    body = functools.partial(_cache_body, scale=size ** (-0.5))
    state = pl.BlockSpec((group * TILE, 1), lambda t, tb: (t, 0))
    spec = pltpu.PrefetchScalarGridSpec(
        num_scalar_prefetch=1,
        grid=(tiles,),
        in_specs=[
            pl.BlockSpec((group, TILE, size), lambda t, tb: (0, t, 0)),
            pl.BlockSpec((TILE, 1), lambda t, tb: (t, 0)),
            pl.BlockSpec(cache.shape, lambda t, tb: (0, 0, 0)),
        ],
        out_specs=[state, state, pl.BlockSpec((group * TILE, size), lambda t, tb: (t, 0))],
    )
    return pl.pallas_call(
        body,
        grid_spec=spec,
        out_shape=[
            jax.ShapeDtypeStruct((group * count, 1), jnp.float32),
            jax.ShapeDtypeStruct((group * count, 1), jnp.float32),
            jax.ShapeDtypeStruct((group * count, size), jnp.float32),
        ],
        compiler_params=pltpu.CompilerParams(dimension_semantics=("arbitrary",)),
    )(tables, q_sorted, req_sorted.reshape(count, 1), cache)


def fresh_attention(tables, q_sorted, o_sorted, rs_sorted, state, kv_sorted):
    group, count, size = q_sorted.shape
    tiles = count // TILE
    body = functools.partial(_fresh_body, scale=size ** (-0.5))
    column = pl.BlockSpec((TILE, 1), lambda t, tb: (t, 0))
    lane = pl.BlockSpec((group * TILE, 1), lambda t, tb: (t, 0))
    spec = pltpu.PrefetchScalarGridSpec(
        num_scalar_prefetch=1,
        grid=(tiles,),
        in_specs=[
            pl.BlockSpec((group, TILE, size), lambda t, tb: (0, t, 0)),
            column,
            column,
            lane,
            lane,
            pl.BlockSpec((group * TILE, size), lambda t, tb: (t, 0)),
            pl.BlockSpec(kv_sorted.shape, lambda t, tb: (0, 0)),
        ],
        out_specs=pl.BlockSpec((group, TILE, size), lambda t, tb: (0, t, 0)),
    )
    return pl.pallas_call(
        body,
        grid_spec=spec,
        out_shape=jax.ShapeDtypeStruct(q_sorted.shape, jnp.bfloat16),
        compiler_params=pltpu.CompilerParams(dimension_semantics=("arbitrary",)),
    )(tables, q_sorted, o_sorted.reshape(count, 1), rs_sorted.reshape(count, 1), *state, kv_sorted)


def rotate_columns(value, shift):
    doubled = jnp.concatenate([value, value], axis=1)
    return lax.dynamic_slice_in_dim(doubled, shift, value.shape[1], axis=1)


def gather_heads(piece):
    parts = lax.psum(1, "heads")
    me = lax.axis_index("heads")
    width = piece.shape[1]
    full = jnp.zeros((piece.shape[0], parts * width), piece.dtype)
    for shift in range(parts):
        got = piece
        if shift > 0:
            pairs = [(i, (i + shift) % parts) for i in range(parts)]
            got = lax.ppermute(piece, "heads", pairs)
        source = lax.rem(me - shift + parts, parts)
        full = lax.dynamic_update_slice_in_dim(full, got, source * width, axis=1)
    return full


def scatter_heads(partial_value):
    parts = lax.psum(1, "heads")
    me = lax.axis_index("heads")
    width = partial_value.shape[1] // parts
    total = lax.dynamic_slice_in_dim(partial_value, me * width, width, axis=1)
    for shift in range(1, parts):
        pairs = [(i, (i + shift) % parts) for i in range(parts)]
        target = lax.rem(me + shift, parts)
        piece = lax.dynamic_slice_in_dim(partial_value, target * width, width, axis=1).astype(jnp.bfloat16)
        total = total + lax.ppermute(piece, "heads", pairs).astype(jnp.float32)
    return total.astype(jnp.bfloat16)


def on_device(
    tokens,
    order,
    lengths,
    block_table,
    destination,
    w_query,
    key_weight,
    value_weight,
    w_out,
    key_value_cache,
):
    local_heads = key_weight.shape[1] // HEAD_SIZE
    slots = destination.shape[0]
    slot_labels = jnp.arange(slots, dtype=jnp.int32)
    inverse = jnp.sum(
        jnp.where(destination[None, :] == slot_labels[:, None], slot_labels[None, :], 0), axis=1
    )
    arranged = jnp.take(key_value_cache, inverse, axis=1)
    layer_zero = key_value_cache[0]
    used = jnp.take(layer_zero, block_table.reshape(-1), axis=0)
    pool, span = used.shape[0], used.shape[1]
    used = used.reshape(pool, span, 2, local_heads, HEAD_SIZE).transpose(0, 1, 3, 2, 4)
    used = used.reshape(pool, span, local_heads * 2 * HEAD_SIZE)
    cache = lax.all_gather(used, "seq", axis=1, tiled=True)
    by_order = jnp.argsort(order)
    full, arranged, by_order = lax.optimization_barrier((gather_heads(tokens), arranged, by_order))
    rows = full.shape[0]
    wide = full.astype(jnp.float32)
    normed = (wide * lax.rsqrt(jnp.mean(wide * wide, axis=1, keepdims=True) + epsilon)).astype(
        jnp.bfloat16
    )
    local_heads = key_weight.shape[1] // HEAD_SIZE
    head_group = QUERY_HEADS // KEY_VALUE_HEADS
    query_rows = jnp.dot(normed, w_query, preferred_element_type=jnp.float32)
    key_rows = jnp.dot(normed, key_weight, preferred_element_type=jnp.float32)
    value_rows = jnp.dot(normed, value_weight, preferred_element_type=jnp.float32)
    device = lax.axis_index("seq")
    my_order = lax.dynamic_slice_in_dim(order, device * rows, rows)
    request, position = request_place(my_order, lengths)
    rotary_angles = (position + CB * BLOCK_POSITIONS).astype(jnp.float32)
    query_rows = apply_rotary(
        query_rows.reshape(rows, local_heads * head_group, HEAD_SIZE), rotary_angles
    ).astype(jnp.bfloat16)
    query_rows = query_rows.reshape(rows, local_heads, head_group, HEAD_SIZE)
    key_rows = (
        apply_rotary(key_rows.reshape(rows, local_heads, HEAD_SIZE), rotary_angles)
        .astype(jnp.bfloat16)
        .reshape(rows, local_heads * HEAD_SIZE)
    )
    fresh_rows = jnp.concatenate(
        [
            key_rows.reshape(rows, local_heads, HEAD_SIZE),
            value_rows.astype(jnp.bfloat16).reshape(rows, local_heads, HEAD_SIZE),
        ],
        axis=2,
    ).reshape(rows, local_heads * 2 * HEAD_SIZE)
    peers = lax.psum(1, "seq")
    spread = jnp.broadcast_to(fresh_rows[None], (peers,) + fresh_rows.shape)
    gathered = lax.all_to_all(spread, "seq", 0, 0, tiled=True).reshape(peers * rows, fresh_rows.shape[1])
    gathered, arranged = lax.optimization_barrier((gathered, arranged))
    decode_cache = lax.all_to_all(arranged, "seq", split_axis=1, concat_axis=2, tiled=True)
    kv_sorted = jnp.take(gathered, by_order, axis=0)
    earlier = (my_order[None, :] < my_order[:, None]).astype(jnp.int32)
    unsort = jnp.sum(earlier, axis=1)
    slots_of = jnp.arange(rows, dtype=jnp.int32)
    perm = jnp.sum(jnp.where(unsort[:, None] == slots_of[None, :], slots_of[:, None], 0), axis=0)
    o_sorted = jnp.take(my_order, perm)
    rs_sorted = jnp.take(my_order - position, perm)
    req_sorted = jnp.take(request, perm)
    q_sorted = jnp.take(query_rows, perm, axis=0)
    tables = attention_tables(o_sorted, rs_sorted, req_sorted)
    outs = []
    for head in range(local_heads):
        q_head = q_sorted[:, head].transpose(1, 0, 2)
        part = slice(head * 2 * HEAD_SIZE, (head + 1) * 2 * HEAD_SIZE)
        state = cache_attention(tables, q_head, req_sorted, cache[:, :, part])
        result = fresh_attention(tables, q_head, o_sorted, rs_sorted, state, kv_sorted[:, part])
        outs.append(result)
    outs = [jnp.take(result, unsort, axis=1).transpose(1, 0, 2) for result in outs]
    attn = jnp.stack(outs, axis=1).reshape(rows, local_heads * head_group * HEAD_SIZE)
    partial_value = jnp.dot(attn, w_out, preferred_element_type=jnp.float32)
    attn_out = scatter_heads(partial_value)
    return (attn_out, decode_cache)


def solution(mesh):
    placed = (
        P("seq", "heads"),
        P(),
        P(),
        P(),
        P(),
        P(None, "heads"),
        P(None, "heads"),
        P(None, "heads"),
        P("heads", None),
        P(None, None, "seq", None, "heads"),
    )
    return jax.shard_map(
        on_device,
        mesh=mesh,
        in_specs=placed,
        out_specs=(P("seq", "heads"), P(None, "seq", None, None, "heads")),
        check_vma=False,
    )
```
